128 devices in a mesh: gx: 4 (over z_lo, core), gy: 32 (over z_hi, x, y).
Axes of the slice: x: 4, y: 4, z: 4 (z_hi: 2, z_lo: 2; z = z_hi * 2 + z_lo), core: 2. Of those that a mesh axis runs over, the one named last changes fastest.
Arguments:
- hidden: bfloat16 [1024, 16384], P('gy'), may hold values from -6 to 6
- norm_gain: bfloat16 [16384], replicated, may hold values from 0.099609375 to 1.8984375
- w_query: bfloat16 [16384, 16384], P('gx', 'gy'), may hold values from -0.046875 to 0.046875
- w_keyval: bfloat16 [16384, 2048], P('gx', 'gy'), may hold values from -0.046875 to 0.046875
- key_cache: bfloat16 [1024, 256, 8, 128], P(('gx', 'gy')), may hold values from -1000 to 1000
- value_cache: bfloat16 [1024, 256, 8, 128], P(('gx', 'gy')), may hold values from -16 to 16
- lengths: int32 [1024], P(('gx', 'gy')), may hold values from 1 to 256, as said below
- w_out: bfloat16 [16384, 16384], P('gy', 'gx'), may hold values from -0.046875 to 0.046875
Outputs:
- mixed: bfloat16 [1024, 16384], P('gy', 'gx')
The draws below stay inside these ranges and needn't reach their ends.
Inputs may be any that keep to these rules, and one draw needn't show every extreme that they name: Slots 0 to lengths - 1 of a row are filled; some row fills all 256.
All inputs are finite; a program needn't handle non-finite values.
Results may differ from the reference program's by a relative error of at most 0.024.
Values may be sent and summed in bfloat16 or wider, within the bound.
No kernel may reach another device: no remote copies, remote signals or barrier semaphores. Data moves between devices by JAX's collectives and lax.ppermute only.
A program may use at most 128 MiB of HBM per device.

```python
import math
import jax
import jax.numpy as jnp
from jax import lax

D = 16384
HEADS = 128
KV_HEADS = 8
HEAD_DIM = 128
CACHE = 256
ROWS = 1024


def draw_key_cache(key, part):
    base_key = jax.random.fold_in(jax.random.fold_in(key, 11), 0)
    shape = (ROWS, CACHE, KV_HEADS, HEAD_DIM)
    base = jnp.clip(jax.random.normal(base_key, shape, jnp.float32), -6.0, 6.0)
    return base.astype(jnp.bfloat16)


def draw_lengths(key, part):
    drawn = jax.random.randint(jax.random.fold_in(key, 23), (ROWS,), 1, CACHE + 1, dtype=jnp.int32)
    return drawn.at[0].set(CACHE)


def block_levels(stream_key, shape, cuts, low, high):
    def one(dim, parts):
        steps = jax.random.uniform(jax.random.fold_in(jax.random.fold_in(stream_key, 6), dim), (parts,), jnp.float32, low / len(cuts), high / len(cuts))
        return jnp.repeat(jnp.exp(steps), shape[dim] // parts).reshape((-1,) + (1,) * (len(shape) - dim - 1))

    factor_of = one(*cuts[0])
    for cut in cuts[1:]:
        factor_of = factor_of * one(*cut)
    return factor_of


def normal_values(stream_key, dims, width, most, cuts=(), kind=jnp.bfloat16):
    values = width * jax.random.normal(stream_key, dims, jnp.float32)
    if cuts:
        values = values * block_levels(stream_key, dims, cuts, -0.22, 0.18)
    return jnp.clip(values, -most, most).astype(kind)


def setup_inputs(seed: int = 0) -> dict:
    key_list = jax.random.split(jax.random.key(seed), 9)
    hidden = normal_values(key_list[0], (ROWS, D), 1.0, 6.0, ((0, 32),))
    norm_gain = jnp.clip(1.0 + 0.18 * jax.random.normal(key_list[1], (D,), jnp.float32), 0.099609375, 1.8984375).astype(jnp.bfloat16)
    w_query = normal_values(key_list[2], (D, HEADS * HEAD_DIM), D ** -0.5, 0.046875, ((0, 4), (1, 32)))
    w_keyval = normal_values(key_list[3], (D, 2 * KV_HEADS * HEAD_DIM), D ** -0.5, 0.046875, ((0, 4), (1, 32)))
    key_cache = draw_key_cache(jax.random.fold_in(key_list[8], 71), 0)
    value_cache = normal_values(key_list[5], (ROWS, CACHE, KV_HEADS, HEAD_DIM), 4.0, 16.0, ((0, 128),))
    lengths = draw_lengths(jax.random.fold_in(key_list[8], 71), 0)
    w_out = normal_values(key_list[7], (HEADS * HEAD_DIM, D), (HEADS * HEAD_DIM) ** -0.5, 0.046875, ((0, 32), (1, 4)))
    return {"hidden": hidden, "norm_gain": norm_gain, "w_query": w_query, "w_keyval": w_keyval, "key_cache": key_cache, "value_cache": value_cache, "lengths": lengths, "w_out": w_out}


def rotate_heads(values, position, head_dim):
    half = head_dim // 2
    freq = jnp.exp(-(jnp.arange(half, dtype=jnp.float32) * 2.0 / head_dim) * math.log(500000.0))
    angle = position[:, None] * freq[None, :]
    cosine = jnp.cos(angle)[:, None, :]
    sine = jnp.sin(angle)[:, None, :]
    first = values[..., :half]
    second = values[..., half:]
    return jnp.concatenate([first * cosine - second * sine, second * cosine + first * sine], axis=-1)

def attend_block(query, keyval, key_block, value_block, length_block):
    rows, cache_len, kv_heads, head_dim = key_block.shape
    heads = query.shape[1] // head_dim
    group = heads // kv_heads
    scale = 1.0 / math.sqrt(head_dim)
    position = length_block.astype(jnp.float32)
    rotated = rotate_heads(query.astype(jnp.float32).reshape(rows, heads, head_dim), position, head_dim).astype(jnp.bfloat16)
    pairs = keyval.reshape(rows, 2, kv_heads, head_dim)
    new_key = rotate_heads(pairs[:, 0].astype(jnp.float32), position, head_dim).astype(jnp.bfloat16)
    new_value = pairs[:, 1].astype(jnp.float32)
    grouped = rotated.astype(jnp.float32).reshape(rows, kv_heads, group, head_dim)
    scores = jnp.einsum('rgqd,rtgd->rgqt', grouped, key_block.astype(jnp.float32)) * scale
    own = jnp.einsum('rgqd,rgd->rgq', grouped, new_key.astype(jnp.float32)) * scale
    valid = jnp.arange(cache_len)[None, None, None, :] < length_block[:, None, None, None]
    scores = jnp.where(valid, scores, -jnp.inf)
    top = jnp.maximum(lax.optimization_barrier(jnp.max(scores, axis=-1)), own)
    weights = jnp.exp(scores - top[..., None])
    own_weight = jnp.exp(own - top)
    total = lax.optimization_barrier(jnp.sum(weights, axis=-1)) + own_weight
    probs = (weights / total[..., None]).astype(jnp.bfloat16)
    own_prob = (own_weight / total).astype(jnp.bfloat16)
    result = jnp.einsum('rgqt,rtgd->rgqd', probs.astype(jnp.float32), value_block.astype(jnp.float32))
    result = result + own_prob.astype(jnp.float32)[..., None] * new_value[:, :, None, :]
    return result.astype(jnp.bfloat16).reshape(rows, heads * head_dim)

def reference(hidden, norm_gain, w_query, w_keyval, key_cache, value_cache, lengths, w_out):
    values = hidden.astype(jnp.float32)
    inverse = lax.rsqrt(lax.optimization_barrier(jnp.mean(values * values, axis=1, keepdims=True)) + 1e-05)
    normed = (values * inverse * norm_gain.astype(jnp.float32)).astype(jnp.bfloat16)
    query = jnp.dot(normed, w_query, preferred_element_type=jnp.float32).astype(jnp.bfloat16)
    keyval = jnp.dot(normed, w_keyval, preferred_element_type=jnp.float32).astype(jnp.bfloat16)
    block = 8
    count = ROWS // block

    def one_block(items):
        return attend_block(*items)
    attended = lax.map(one_block, (query.reshape(count, block, query.shape[1]), keyval.reshape(count, block, keyval.shape[1]), key_cache.reshape((count, block) + key_cache.shape[1:]), value_cache.reshape((count, block) + value_cache.shape[1:]), lengths.reshape(count, block)))
    attended = attended.reshape(ROWS, HEADS * HEAD_DIM)
    return jnp.dot(attended, w_out, preferred_element_type=jnp.float32).astype(jnp.bfloat16)
```

```python
import math

import jax
import jax.numpy as jnp
from jax import lax
from jax.sharding import PartitionSpec as P

GY = ("zh", "x", "y")


def rotate_heads(values, position, head_dim):
    half = head_dim // 2
    freq = jnp.exp(-(jnp.arange(half, dtype=jnp.float32) * 2.0 / head_dim) * math.log(500000.0))
    angle = position[:, None] * freq[None, :]
    cosine = jnp.cos(angle)[:, None, :]
    sine = jnp.sin(angle)[:, None, :]
    first = values[..., :half]
    second = values[..., half:]
    return jnp.concatenate(
        [first * cosine - second * sine, second * cosine + first * sine], axis=-1
    )


def attend_rows(query, keyval, key_cache, value_cache, lengths):
    rows, cache_len, kv_heads, head_dim = key_cache.shape
    heads = query.shape[1] // head_dim
    group = heads // kv_heads
    scale = 1.0 / math.sqrt(head_dim)
    position = lengths.astype(jnp.float32)
    rotated = rotate_heads(
        query.astype(jnp.float32).reshape(rows, heads, head_dim), position, head_dim
    ).astype(jnp.bfloat16)
    pairs = keyval.reshape(rows, 2, kv_heads, head_dim)
    new_key = rotate_heads(pairs[:, 0].astype(jnp.float32), position, head_dim).astype(jnp.bfloat16)
    new_value = pairs[:, 1].astype(jnp.float32)
    grouped = rotated.reshape(rows, kv_heads, group, head_dim)
    scores = (
        jnp.einsum("rgqd,rtgd->rgqt", grouped, key_cache, preferred_element_type=jnp.float32)
        * scale
    )
    own = jnp.einsum("rgqd,rgd->rgq", grouped, new_key, preferred_element_type=jnp.float32) * scale
    valid = jnp.arange(cache_len)[None, None, None, :] < lengths[:, None, None, None]
    scores = jnp.where(valid, scores, -jnp.inf)
    top = jnp.maximum(jnp.max(scores, axis=-1), own)
    weights = jnp.exp(scores - top[..., None])
    own_weight = jnp.exp(own - top)
    total = jnp.sum(weights, axis=-1) + own_weight
    probs = (weights / total[..., None]).astype(jnp.bfloat16)
    own_prob = (own_weight / total).astype(jnp.bfloat16)
    result = jnp.einsum("rgqt,rtgd->rgqd", probs, value_cache, preferred_element_type=jnp.float32)
    result = result + own_prob.astype(jnp.float32)[..., None] * new_value[:, :, None, :]
    return result.astype(jnp.bfloat16).reshape(rows, heads * head_dim)


def shards(hidden, norm_gain, w_query, w_keyval, key_cache, value_cache, lengths, w_out):
    width_part = w_query.shape[0]
    query_cols = w_query.shape[1]
    pair_cols = w_keyval.shape[1]
    peers = 32
    values = hidden.astype(jnp.float32)
    inverse = lax.rsqrt(jnp.mean(values * values, axis=1, keepdims=True) + 1e-05)
    normed = (values * inverse * norm_gain.astype(jnp.float32)).astype(jnp.bfloat16)
    own_cols = lax.dynamic_slice_in_dim(normed, lax.axis_index("gx") * width_part, width_part, 1)
    gathered = lax.all_gather(own_cols, GY, axis=0, tiled=True)
    summed = lax.psum_scatter(
        jnp.concatenate(
            [
                jnp.dot(gathered, w_query, preferred_element_type=jnp.float32),
                jnp.dot(gathered, w_keyval, preferred_element_type=jnp.float32),
            ],
            axis=1,
        ),
        "gx",
        scatter_dimension=0,
        tiled=True,
    )
    packed = summed.astype(jnp.bfloat16)
    local_qkv = lax.all_to_all(packed, GY, split_axis=0, concat_axis=1, tiled=True)
    rows_dev = local_qkv.shape[0]
    split_cols = local_qkv.reshape(rows_dev, peers, query_cols + pair_cols)
    query = split_cols[:, :, :query_cols].reshape(rows_dev, peers * query_cols)
    keyval = split_cols[:, :, query_cols:].reshape(rows_dev, peers * pair_cols)
    attended = attend_rows(query, keyval, key_cache, value_cache, lengths)
    by_heads = lax.all_to_all(attended, GY, split_axis=1, concat_axis=0, tiled=True)
    full_rows = lax.all_gather(by_heads, "gx", axis=0, tiled=True)
    full_rows = full_rows.reshape(2, 4, 4, -1, full_rows.shape[1]).transpose(2, 1, 0, 3, 4)
    full_rows = full_rows.reshape(-1, full_rows.shape[-1])
    partial_out = jnp.dot(full_rows, w_out, preferred_element_type=jnp.float32)
    part = partial_out.astype(jnp.bfloat16)
    rows, cols = part.shape
    part = lax.psum_scatter(part, "y", scatter_dimension=0, tiled=True)
    part = lax.psum_scatter(part, "x", scatter_dimension=0, tiled=True)
    part = lax.psum_scatter(part, "zh", scatter_dimension=0, tiled=True)
    return part.reshape(rows // 32, cols)


def solution(mesh):
    from jax.sharding import Mesh
    mesh = Mesh(mesh.devices.reshape(4, 2, 4, 4), ("gx", "zh", "x", "y"))
    in_specs = (
        P(GY, None),
        P(),
        P("gx", GY),
        P("gx", GY),
        P(("gx",) + GY, None, None, None),
        P(("gx",) + GY, None, None, None),
        P(("gx",) + GY),
        P(GY, "gx"),
    )
    out_specs = P(GY, "gx")
    return jax.shard_map(shards, mesh=mesh, in_specs=in_specs, out_specs=out_specs, check_vma=False)
```

```python
import math

import jax
import jax.numpy as jnp
from jax import lax
from jax.sharding import PartitionSpec as P

GY = ("zh", "x", "y")


def rotate_heads(values, position, head_dim):
    half = head_dim // 2
    freq = jnp.exp(-(jnp.arange(half, dtype=jnp.float32) * 2.0 / head_dim) * math.log(500000.0))
    angle = position[:, None] * freq[None, :]
    cosine = jnp.cos(angle)[:, None, :]
    sine = jnp.sin(angle)[:, None, :]
    first = values[..., :half]
    second = values[..., half:]
    return jnp.concatenate(
        [first * cosine - second * sine, second * cosine + first * sine], axis=-1
    )


def attend_rows(query, keyval, key_cache, value_cache, lengths):
    rows, cache_len, kv_heads, head_dim = key_cache.shape
    heads = query.shape[1] // head_dim
    group = heads // kv_heads
    scale = 1.0 / math.sqrt(head_dim)
    position = lengths.astype(jnp.float32)
    rotated = rotate_heads(
        query.astype(jnp.float32).reshape(rows, heads, head_dim), position, head_dim
    ).astype(jnp.bfloat16)
    pairs = keyval.reshape(rows, 2, kv_heads, head_dim)
    new_key = rotate_heads(pairs[:, 0].astype(jnp.float32), position, head_dim).astype(jnp.bfloat16)
    new_value = pairs[:, 1].astype(jnp.float32)
    grouped = rotated.reshape(rows, kv_heads, group, head_dim)
    scores = (
        jnp.einsum("rgqd,rtgd->rgqt", grouped, key_cache, preferred_element_type=jnp.float32)
        * scale
    )
    own = jnp.einsum("rgqd,rgd->rgq", grouped, new_key, preferred_element_type=jnp.float32) * scale
    valid = jnp.arange(cache_len)[None, None, None, :] < lengths[:, None, None, None]
    scores = jnp.where(valid, scores, -jnp.inf)
    top = jnp.maximum(jnp.max(scores, axis=-1), own)
    weights = jnp.exp(scores - top[..., None])
    own_weight = jnp.exp(own - top)
    total = jnp.sum(weights, axis=-1) + own_weight
    probs = (weights / total[..., None]).astype(jnp.bfloat16)
    own_prob = (own_weight / total).astype(jnp.bfloat16)
    result = jnp.einsum("rgqt,rtgd->rgqd", probs, value_cache, preferred_element_type=jnp.float32)
    result = result + own_prob.astype(jnp.float32)[..., None] * new_value[:, :, None, :]
    return result.astype(jnp.bfloat16).reshape(rows, heads * head_dim)


def shards(hidden, norm_gain, w_query, w_keyval, key_cache, value_cache, lengths, w_out):
    width_part = w_query.shape[0]
    query_cols = w_query.shape[1]
    pair_cols = w_keyval.shape[1]
    peers = 32
    values = hidden.astype(jnp.float32)
    inverse = lax.rsqrt(jnp.mean(values * values, axis=1, keepdims=True) + 1e-05)
    normed = (values * inverse * norm_gain.astype(jnp.float32)).astype(jnp.bfloat16)
    own_cols = lax.dynamic_slice_in_dim(normed, lax.axis_index("gx") * width_part, width_part, 1)
    gathered = lax.all_gather(own_cols, "zh", axis=0, tiled=True)
    gathered = lax.all_gather(gathered, ("x", "y"), axis=0, tiled=True)
    projected = jnp.concatenate(
        [
            jnp.dot(gathered, w_query, preferred_element_type=jnp.float32),
            jnp.dot(gathered, w_keyval, preferred_element_type=jnp.float32),
        ],
        axis=1,
    )
    projected = projected.reshape(4, 4, 2, -1, projected.shape[1]).transpose(2, 0, 1, 3, 4)
    projected = projected.reshape(-1, projected.shape[-1])
    summed = lax.psum_scatter(projected, "gx", scatter_dimension=0, tiled=True)
    packed = summed.astype(jnp.bfloat16)
    local_qkv = lax.all_to_all(packed, GY, split_axis=0, concat_axis=1, tiled=True)
    rows_dev = local_qkv.shape[0]
    split_cols = local_qkv.reshape(rows_dev, peers, query_cols + pair_cols)
    query = split_cols[:, :, :query_cols].reshape(rows_dev, peers * query_cols)
    keyval = split_cols[:, :, query_cols:].reshape(rows_dev, peers * pair_cols)
    attended = attend_rows(query, keyval, key_cache, value_cache, lengths)
    by_heads = lax.all_to_all(attended, GY, split_axis=1, concat_axis=0, tiled=True)
    full_rows = lax.all_gather(by_heads, "gx", axis=0, tiled=True)
    partial_out = jnp.dot(full_rows, w_out, preferred_element_type=jnp.float32)
    part = partial_out.astype(jnp.bfloat16)
    rows, cols = part.shape
    part = lax.all_to_all(part, GY, split_axis=0, concat_axis=0, tiled=True)
    part = part.reshape(peers, rows // peers, cols).astype(jnp.float32).sum(axis=0)
    return part.astype(jnp.bfloat16)


def solution(mesh):
    from jax.sharding import Mesh
    mesh = Mesh(mesh.devices.reshape(4, 2, 4, 4), ("gx", "zh", "x", "y"))
    in_specs = (
        P(GY, None),
        P(),
        P("gx", GY),
        P("gx", GY),
        P(("gx",) + GY, None, None, None),
        P(("gx",) + GY, None, None, None),
        P(("gx",) + GY),
        P(GY, "gx"),
    )
    out_specs = P(GY, "gx")
    return jax.shard_map(shards, mesh=mesh, in_specs=in_specs, out_specs=out_specs, check_vma=False)
```

```python
import math

import jax
import jax.numpy as jnp
from jax import lax
from jax.sharding import PartitionSpec as P

GY = ("zh", "x", "y")
ALL = ("gx",) + GY


def rotate_heads(values, position, head_dim):
    half = head_dim // 2
    freq = jnp.exp(-(jnp.arange(half, dtype=jnp.float32) * 2.0 / head_dim) * math.log(500000.0))
    angle = position[:, None] * freq[None, :]
    cosine = jnp.cos(angle)[:, None, :]
    sine = jnp.sin(angle)[:, None, :]
    first = values[..., :half]
    second = values[..., half:]
    return jnp.concatenate(
        [first * cosine - second * sine, second * cosine + first * sine], axis=-1
    )


def attend_rows(query, keyval, key_cache, value_cache, lengths):
    rows, cache_len, kv_heads, head_dim = key_cache.shape
    heads = query.shape[1] // head_dim
    group = heads // kv_heads
    scale = 1.0 / math.sqrt(head_dim)
    position = lengths.astype(jnp.float32)
    rotated = rotate_heads(
        query.astype(jnp.float32).reshape(rows, heads, head_dim), position, head_dim
    ).astype(jnp.bfloat16)
    pairs = keyval.reshape(rows, 2, kv_heads, head_dim)
    new_key = rotate_heads(pairs[:, 0].astype(jnp.float32), position, head_dim).astype(jnp.bfloat16)
    new_value = pairs[:, 1].astype(jnp.float32)
    grouped = rotated.reshape(rows, kv_heads, group, head_dim)
    scores = (
        jnp.einsum("rgqd,rtgd->rgqt", grouped, key_cache, preferred_element_type=jnp.float32)
        * scale
    )
    own = jnp.einsum("rgqd,rgd->rgq", grouped, new_key, preferred_element_type=jnp.float32) * scale
    valid = jnp.arange(cache_len)[None, None, None, :] < lengths[:, None, None, None]
    scores = jnp.where(valid, scores, -jnp.inf)
    top = jnp.maximum(jnp.max(scores, axis=-1), own)
    weights = jnp.exp(scores - top[..., None])
    own_weight = jnp.exp(own - top)
    total = jnp.sum(weights, axis=-1) + own_weight
    probs = (weights / total[..., None]).astype(jnp.bfloat16)
    own_prob = (own_weight / total).astype(jnp.bfloat16)
    result = jnp.einsum("rgqt,rtgd->rgqd", probs, value_cache, preferred_element_type=jnp.float32)
    result = result + own_prob.astype(jnp.float32)[..., None] * new_value[:, :, None, :]
    return result.astype(jnp.bfloat16).reshape(rows, heads * head_dim)


def shards(hidden, norm_gain, w_query, w_keyval, key_cache, value_cache, lengths, w_out):
    width_part = w_query.shape[0]
    query_cols = w_query.shape[1]
    pair_cols = w_keyval.shape[1]
    peers = 32
    values = hidden.astype(jnp.float32)
    inverse = lax.rsqrt(jnp.mean(values * values, axis=1, keepdims=True) + 1e-05)
    normed = (values * inverse * norm_gain.astype(jnp.float32)).astype(jnp.bfloat16)
    own_cols = lax.dynamic_slice_in_dim(normed, lax.axis_index("gx") * width_part, width_part, 1)
    gathered = lax.all_gather(own_cols, "zh", axis=0, tiled=True)
    gathered = lax.all_gather(gathered, ("x", "y"), axis=0, tiled=True)
    projected = jnp.concatenate(
        [
            jnp.dot(gathered, w_query, preferred_element_type=jnp.float32),
            jnp.dot(gathered, w_keyval, preferred_element_type=jnp.float32),
        ],
        axis=1,
    )
    projected = projected.reshape(4, 4, 2, -1, projected.shape[1]).transpose(2, 0, 1, 3, 4)
    projected = projected.reshape(-1, projected.shape[-1])
    arrived = lax.all_to_all(projected, ALL, split_axis=0, concat_axis=0, tiled=True)
    rows_dev = arrived.shape[0] // 128
    summed = arrived.reshape(4, peers, rows_dev, query_cols + pair_cols).sum(axis=0)
    split_cols = summed.astype(jnp.bfloat16).transpose(1, 0, 2)
    query = split_cols[:, :, :query_cols].reshape(rows_dev, peers * query_cols)
    keyval = split_cols[:, :, query_cols:].reshape(rows_dev, peers * pair_cols)
    attended = attend_rows(query, keyval, key_cache, value_cache, lengths)
    heads_first = attended.reshape(rows_dev, peers, query_cols).transpose(1, 0, 2)
    sent = jnp.broadcast_to(heads_first[None], (4,) + heads_first.shape).reshape(-1, query_cols)
    full_rows = lax.all_to_all(sent, ALL, split_axis=0, concat_axis=0, tiled=True)
    partial_out = jnp.dot(full_rows, w_out, preferred_element_type=jnp.float32)
    part = partial_out.astype(jnp.bfloat16)
    rows, cols = part.shape
    part = lax.all_to_all(part, GY, split_axis=0, concat_axis=0, tiled=True)
    part = part.reshape(peers, rows // peers, cols).astype(jnp.float32).sum(axis=0)
    return part.astype(jnp.bfloat16)


def solution(mesh):
    from jax.sharding import Mesh
    mesh = Mesh(mesh.devices.reshape(4, 2, 4, 4), ("gx", "zh", "x", "y"))
    in_specs = (
        P(GY, None),
        P(),
        P("gx", GY),
        P("gx", GY),
        P(("gx",) + GY, None, None, None),
        P(("gx",) + GY, None, None, None),
        P(("gx",) + GY),
        P(GY, "gx"),
    )
    out_specs = P(GY, "gx")
    return jax.shard_map(shards, mesh=mesh, in_specs=in_specs, out_specs=out_specs, check_vma=False)
```

```python
import math

import jax
import jax.numpy as jnp
from jax import lax
from jax.sharding import PartitionSpec as P

GY = ("zh", "x", "y")
ALL = ("gx",) + GY


def rotate_heads(values, position, head_dim):
    half = head_dim // 2
    freq = jnp.exp(-(jnp.arange(half, dtype=jnp.float32) * 2.0 / head_dim) * math.log(500000.0))
    angle = position[:, None] * freq[None, :]
    cosine = jnp.cos(angle)[:, None, :]
    sine = jnp.sin(angle)[:, None, :]
    first = values[..., :half]
    second = values[..., half:]
    return jnp.concatenate(
        [first * cosine - second * sine, second * cosine + first * sine], axis=-1
    )


def attend_rows(query, keyval, key_cache, value_cache, lengths):
    rows, cache_len, kv_heads, head_dim = key_cache.shape
    heads = query.shape[1] // head_dim
    group = heads // kv_heads
    scale = 1.0 / math.sqrt(head_dim)
    position = lengths.astype(jnp.float32)
    rotated = rotate_heads(
        query.astype(jnp.float32).reshape(rows, heads, head_dim), position, head_dim
    ).astype(jnp.bfloat16)
    pairs = keyval.reshape(rows, 2, kv_heads, head_dim)
    new_key = rotate_heads(pairs[:, 0].astype(jnp.float32), position, head_dim).astype(jnp.bfloat16)
    new_value = pairs[:, 1].astype(jnp.float32)
    grouped = rotated.reshape(rows, kv_heads, group, head_dim)
    scores = (
        jnp.einsum("rgqd,rtgd->rgqt", grouped, key_cache, preferred_element_type=jnp.float32)
        * scale
    )
    own = jnp.einsum("rgqd,rgd->rgq", grouped, new_key, preferred_element_type=jnp.float32) * scale
    valid = jnp.arange(cache_len)[None, None, None, :] < lengths[:, None, None, None]
    scores = jnp.where(valid, scores, -jnp.inf)
    top = jnp.maximum(jnp.max(scores, axis=-1), own)
    weights = jnp.exp(scores - top[..., None])
    own_weight = jnp.exp(own - top)
    total = jnp.sum(weights, axis=-1) + own_weight
    probs = (weights / total[..., None]).astype(jnp.bfloat16)
    own_prob = (own_weight / total).astype(jnp.bfloat16)
    result = jnp.einsum("rgqt,rtgd->rgqd", probs, value_cache, preferred_element_type=jnp.float32)
    result = result + own_prob.astype(jnp.float32)[..., None] * new_value[:, :, None, :]
    return result.astype(jnp.bfloat16).reshape(rows, heads * head_dim)


def ring_reduce_scatter(arr, axis, dim):
    n = arr.shape[dim]
    idx = lax.axis_index(axis)
    half = arr.shape[-1] // 2
    cw, ccw = arr[..., :half], arr[..., half:]

    def take(a, k):
        return lax.dynamic_index_in_dim(a, k % n, dim, keepdims=False)

    fwd = [(i, (i + 1) % n) for i in range(n)]
    bwd = [(i, (i - 1) % n) for i in range(n)]
    acc_cw, acc_ccw = take(cw, idx - 1), take(ccw, idx + 1)
    for s in range(n - 1):
        acc_cw = lax.ppermute(acc_cw, axis, fwd) + take(cw, idx - s - 2)
        acc_ccw = lax.ppermute(acc_ccw, axis, bwd) + take(ccw, idx + s + 2)
    return jnp.concatenate([acc_cw, acc_ccw], axis=-1)


def shards(hidden, norm_gain, w_query, w_keyval, key_cache, value_cache, lengths, w_out):
    width_part = w_query.shape[0]
    query_cols = w_query.shape[1]
    pair_cols = w_keyval.shape[1]
    peers = 32
    values = hidden.astype(jnp.float32)
    inverse = lax.rsqrt(jnp.mean(values * values, axis=1, keepdims=True) + 1e-05)
    normed = (values * inverse * norm_gain.astype(jnp.float32)).astype(jnp.bfloat16)
    own_cols = lax.dynamic_slice_in_dim(normed, lax.axis_index("gx") * width_part, width_part, 1)
    gathered = lax.all_gather(own_cols, "zh", axis=0, tiled=True)
    gathered = lax.all_gather(gathered, ("x", "y"), axis=0, tiled=True)
    projected = jnp.concatenate(
        [
            jnp.dot(gathered, w_query, preferred_element_type=jnp.float32),
            jnp.dot(gathered, w_keyval, preferred_element_type=jnp.float32),
        ],
        axis=1,
    )
    projected = projected.reshape(4, 4, 2, -1, projected.shape[1]).transpose(2, 0, 1, 3, 4)
    projected = projected.reshape(-1, projected.shape[-1])
    arrived = lax.all_to_all(projected.astype(jnp.bfloat16), ALL, split_axis=0, concat_axis=0, tiled=True)
    rows_dev = arrived.shape[0] // 128
    summed = arrived.reshape(4, peers, rows_dev, query_cols + pair_cols).astype(jnp.float32).sum(axis=0)
    split_cols = summed.astype(jnp.bfloat16).transpose(1, 0, 2)
    query = split_cols[:, :, :query_cols].reshape(rows_dev, peers * query_cols)
    keyval = split_cols[:, :, query_cols:].reshape(rows_dev, peers * pair_cols)
    attended = attend_rows(query, keyval, key_cache, value_cache, lengths)
    heads_first = attended.reshape(rows_dev, peers, query_cols).transpose(1, 0, 2)
    sent = jnp.broadcast_to(heads_first[None], (4,) + heads_first.shape).reshape(-1, query_cols)
    full_rows = lax.all_to_all(sent, ALL, split_axis=0, concat_axis=0, tiled=True)
    partial_out = jnp.dot(full_rows, w_out, preferred_element_type=jnp.float32)
    part = partial_out.astype(jnp.bfloat16)
    rows, cols = part.shape
    part = part.reshape(2, 4, 4, rows // peers, cols)
    first, second = part[..., : cols // 2], part[..., cols // 2 :]
    first = ring_reduce_scatter(first, "y", 2)
    second = ring_reduce_scatter(second, "x", 1)
    first = ring_reduce_scatter(first, "x", 1)
    second = ring_reduce_scatter(second, "y", 1)
    first = ring_reduce_scatter(first, "zh", 0)
    second = ring_reduce_scatter(second, "zh", 0)
    return jnp.concatenate([first, second], axis=-1)


def solution(mesh):
    from jax.sharding import Mesh
    mesh = Mesh(mesh.devices.reshape(4, 2, 4, 4), ("gx", "zh", "x", "y"))
    in_specs = (
        P(GY, None),
        P(),
        P("gx", GY),
        P("gx", GY),
        P(("gx",) + GY, None, None, None),
        P(("gx",) + GY, None, None, None),
        P(("gx",) + GY),
        P(GY, "gx"),
    )
    out_specs = P(GY, "gx")
    return jax.shard_map(shards, mesh=mesh, in_specs=in_specs, out_specs=out_specs, check_vma=False)
```

```python
import math

import jax
import jax.numpy as jnp
from jax import lax
from jax.sharding import PartitionSpec as P

GY = ("zh", "x", "y")
ALL = ("gx",) + GY


def rotate_heads(values, position, head_dim):
    half = head_dim // 2
    freq = jnp.exp(-(jnp.arange(half, dtype=jnp.float32) * 2.0 / head_dim) * math.log(500000.0))
    angle = position[:, None] * freq[None, :]
    cosine = jnp.cos(angle)[:, None, :]
    sine = jnp.sin(angle)[:, None, :]
    first = values[..., :half]
    second = values[..., half:]
    return jnp.concatenate(
        [first * cosine - second * sine, second * cosine + first * sine], axis=-1
    )


def attend_rows(query, keyval, key_cache, value_cache, lengths):
    rows, cache_len, kv_heads, head_dim = key_cache.shape
    heads = query.shape[1] // head_dim
    group = heads // kv_heads
    scale = 1.0 / math.sqrt(head_dim)
    position = lengths.astype(jnp.float32)
    rotated = rotate_heads(
        query.astype(jnp.float32).reshape(rows, heads, head_dim), position, head_dim
    ).astype(jnp.bfloat16)
    pairs = keyval.reshape(rows, 2, kv_heads, head_dim)
    new_key = rotate_heads(pairs[:, 0].astype(jnp.float32), position, head_dim).astype(jnp.bfloat16)
    new_value = pairs[:, 1].astype(jnp.float32)
    grouped = rotated.reshape(rows, kv_heads, group, head_dim)
    scores = (
        jnp.einsum("rgqd,rtgd->rgqt", grouped, key_cache, preferred_element_type=jnp.float32)
        * scale
    )
    own = jnp.einsum("rgqd,rgd->rgq", grouped, new_key, preferred_element_type=jnp.float32) * scale
    valid = jnp.arange(cache_len)[None, None, None, :] < lengths[:, None, None, None]
    scores = jnp.where(valid, scores, -jnp.inf)
    top = jnp.maximum(jnp.max(scores, axis=-1), own)
    weights = jnp.exp(scores - top[..., None])
    own_weight = jnp.exp(own - top)
    total = jnp.sum(weights, axis=-1) + own_weight
    probs = (weights / total[..., None]).astype(jnp.bfloat16)
    own_prob = (own_weight / total).astype(jnp.bfloat16)
    result = jnp.einsum("rgqt,rtgd->rgqd", probs, value_cache, preferred_element_type=jnp.float32)
    result = result + own_prob.astype(jnp.float32)[..., None] * new_value[:, :, None, :]
    return result.astype(jnp.bfloat16).reshape(rows, heads * head_dim)


def ring_all_gather(blk, axis, n, dim):
    idx = lax.axis_index(axis)
    half = blk.shape[-1] // 2
    pieces = []
    for part, step in ((blk[..., :half], 1), (blk[..., half:], -1)):
        perm = [(i, (i + step) % n) for i in range(n)]
        out = jnp.zeros(part.shape[:dim] + (n,) + part.shape[dim:], part.dtype)
        out = lax.dynamic_update_index_in_dim(out, part, idx, dim)
        for s in range(1, n):
            part = lax.ppermute(part, axis, perm)
            out = lax.dynamic_update_index_in_dim(out, part, (idx - step * s) % n, dim)
        pieces.append(out)
    return jnp.concatenate(pieces, axis=-1)


def ring_reduce_scatter(arr, axis, dim):
    n = arr.shape[dim]
    idx = lax.axis_index(axis)
    half = arr.shape[-1] // 2
    cw, ccw = arr[..., :half], arr[..., half:]

    def take(a, k):
        return lax.dynamic_index_in_dim(a, k % n, dim, keepdims=False)

    fwd = [(i, (i + 1) % n) for i in range(n)]
    bwd = [(i, (i - 1) % n) for i in range(n)]
    acc_cw, acc_ccw = take(cw, idx - 1), take(ccw, idx + 1)
    for s in range(n - 1):
        acc_cw = lax.ppermute(acc_cw, axis, fwd) + take(cw, idx - s - 2)
        acc_ccw = lax.ppermute(acc_ccw, axis, bwd) + take(ccw, idx + s + 2)
    return jnp.concatenate([acc_cw, acc_ccw], axis=-1)


def shards(hidden, norm_gain, w_query, w_keyval, key_cache, value_cache, lengths, w_out):
    width_part = w_query.shape[0]
    query_cols = w_query.shape[1]
    pair_cols = w_keyval.shape[1]
    peers = 32
    values = hidden.astype(jnp.float32)
    inverse = lax.rsqrt(jnp.mean(values * values, axis=1, keepdims=True) + 1e-05)
    normed = (values * inverse * norm_gain.astype(jnp.float32)).astype(jnp.bfloat16)
    own_cols = lax.dynamic_slice_in_dim(normed, lax.axis_index("gx") * width_part, width_part, 1)
    pair = lax.all_gather(own_cols, "zh", axis=0, tiled=False)
    first = pair[..., : width_part // 2]
    second = pair[..., width_part // 2 :]
    first = ring_all_gather(first, "y", 4, 0)
    second = ring_all_gather(second, "x", 4, 0)
    first = ring_all_gather(first, "x", 4, 0)
    second = ring_all_gather(second, "y", 4, 1)
    gathered = jnp.concatenate([first, second], axis=-1).reshape(-1, width_part)
    projected = jnp.concatenate(
        [
            jnp.dot(gathered, w_query, preferred_element_type=jnp.float32),
            jnp.dot(gathered, w_keyval, preferred_element_type=jnp.float32),
        ],
        axis=1,
    )
    projected = projected.reshape(4, 4, 2, -1, projected.shape[1]).transpose(2, 0, 1, 3, 4)
    projected = projected.reshape(-1, projected.shape[-1])
    arrived = lax.all_to_all(projected.astype(jnp.bfloat16), ALL, split_axis=0, concat_axis=0, tiled=True)
    rows_dev = arrived.shape[0] // 128
    summed = arrived.reshape(4, peers, rows_dev, query_cols + pair_cols).astype(jnp.float32).sum(axis=0)
    split_cols = summed.astype(jnp.bfloat16).transpose(1, 0, 2)
    query = split_cols[:, :, :query_cols].reshape(rows_dev, peers * query_cols)
    keyval = split_cols[:, :, query_cols:].reshape(rows_dev, peers * pair_cols)
    attended = attend_rows(query, keyval, key_cache, value_cache, lengths)
    heads_first = attended.reshape(rows_dev, peers, query_cols).transpose(1, 0, 2)
    sent = jnp.broadcast_to(heads_first[None], (4,) + heads_first.shape).reshape(-1, query_cols)
    full_rows = lax.all_to_all(sent, ALL, split_axis=0, concat_axis=0, tiled=True)
    partial_out = jnp.dot(full_rows, w_out, preferred_element_type=jnp.float32)
    part = partial_out.astype(jnp.bfloat16)
    rows, cols = part.shape
    part = part.reshape(2, 4, 4, rows // peers, cols)
    first, second = part[..., : cols // 2], part[..., cols // 2 :]
    first = ring_reduce_scatter(first, "y", 2)
    second = ring_reduce_scatter(second, "x", 1)
    first = ring_reduce_scatter(first, "x", 1)
    second = ring_reduce_scatter(second, "y", 1)
    first = ring_reduce_scatter(first, "zh", 0)
    second = ring_reduce_scatter(second, "zh", 0)
    return jnp.concatenate([first, second], axis=-1)


def solution(mesh):
    from jax.sharding import Mesh
    mesh = Mesh(mesh.devices.reshape(4, 2, 4, 4), ("gx", "zh", "x", "y"))
    in_specs = (
        P(GY, None),
        P(),
        P("gx", GY),
        P("gx", GY),
        P(("gx",) + GY, None, None, None),
        P(("gx",) + GY, None, None, None),
        P(("gx",) + GY),
        P(GY, "gx"),
    )
    out_specs = P(GY, "gx")
    return jax.shard_map(shards, mesh=mesh, in_specs=in_specs, out_specs=out_specs, check_vma=False)
```

```python
import math

import jax
import jax.numpy as jnp
from jax import lax
from jax.sharding import PartitionSpec as P

GY = ("zh", "x", "y")
ALL = ("gx",) + GY


def rotate_heads(values, position, head_dim):
    half = head_dim // 2
    freq = jnp.exp(-(jnp.arange(half, dtype=jnp.float32) * 2.0 / head_dim) * math.log(500000.0))
    angle = position[:, None] * freq[None, :]
    cosine = jnp.cos(angle)[:, None, :]
    sine = jnp.sin(angle)[:, None, :]
    first = values[..., :half]
    second = values[..., half:]
    return jnp.concatenate(
        [first * cosine - second * sine, second * cosine + first * sine], axis=-1
    )


def attend_rows(query, keyval, key_cache, value_cache, lengths):
    rows, cache_len, kv_heads, head_dim = key_cache.shape
    heads = query.shape[1] // head_dim
    group = heads // kv_heads
    scale = 1.0 / math.sqrt(head_dim)
    position = lengths.astype(jnp.float32)
    rotated = rotate_heads(
        query.astype(jnp.float32).reshape(rows, heads, head_dim), position, head_dim
    ).astype(jnp.bfloat16)
    pairs = keyval.reshape(rows, 2, kv_heads, head_dim)
    new_key = rotate_heads(pairs[:, 0].astype(jnp.float32), position, head_dim).astype(jnp.bfloat16)
    new_value = pairs[:, 1].astype(jnp.float32)
    grouped = rotated.reshape(rows, kv_heads, group, head_dim)
    scores = (
        jnp.einsum("rgqd,rtgd->rgqt", grouped, key_cache, preferred_element_type=jnp.float32)
        * scale
    )
    own = jnp.einsum("rgqd,rgd->rgq", grouped, new_key, preferred_element_type=jnp.float32) * scale
    valid = jnp.arange(cache_len)[None, None, None, :] < lengths[:, None, None, None]
    scores = jnp.where(valid, scores, -jnp.inf)
    top = jnp.maximum(jnp.max(scores, axis=-1), own)
    weights = jnp.exp(scores - top[..., None])
    own_weight = jnp.exp(own - top)
    total = jnp.sum(weights, axis=-1) + own_weight
    probs = (weights / total[..., None]).astype(jnp.bfloat16)
    own_prob = (own_weight / total).astype(jnp.bfloat16)
    result = jnp.einsum("rgqt,rtgd->rgqd", probs, value_cache, preferred_element_type=jnp.float32)
    result = result + own_prob.astype(jnp.float32)[..., None] * new_value[:, :, None, :]
    return result.astype(jnp.bfloat16).reshape(rows, heads * head_dim)


def ring_all_gather(blk, axis, n, dim):
    idx = lax.axis_index(axis)
    fwd = [(i, (i + 1) % n) for i in range(n)]
    bwd = [(i, (i - 1) % n) for i in range(n)]
    out = jnp.zeros(blk.shape[:dim] + (n,) + blk.shape[dim:], blk.dtype)
    out = lax.dynamic_update_index_in_dim(out, blk, idx, dim)
    from_left = lax.ppermute(blk, axis, fwd)
    out = lax.dynamic_update_index_in_dim(out, from_left, (idx - 1) % n, dim)
    if n == 2:
        return out
    from_right = lax.ppermute(blk, axis, bwd)
    out = lax.dynamic_update_index_in_dim(out, from_right, (idx + 1) % n, dim)
    half = blk.shape[-1] // 2
    first = lax.ppermute(from_left[..., :half], axis, fwd)
    second = lax.ppermute(from_right[..., half:], axis, bwd)
    opposite = jnp.concatenate([first, second], axis=-1)
    return lax.dynamic_update_index_in_dim(out, opposite, (idx + 2) % n, dim)


def ring_reduce_scatter(arr, axis, dim):
    n = arr.shape[dim]
    idx = lax.axis_index(axis)

    def take(k):
        return lax.dynamic_index_in_dim(arr, k % n, dim, keepdims=False)

    fwd = [(i, (i + 1) % n) for i in range(n)]
    bwd = [(i, (i - 1) % n) for i in range(n)]
    if n == 2:
        return take(idx) + lax.ppermute(take(idx + 1), axis, fwd)
    half = arr.shape[-1] // 2
    opposite = take(idx + 2)
    from_right = lax.ppermute(opposite[..., :half], axis, bwd)
    from_left = lax.ppermute(opposite[..., half:], axis, fwd)
    to_left = take(idx - 1)
    to_left = jnp.concatenate([to_left[..., :half] + from_right, to_left[..., half:]], axis=-1)
    to_right = take(idx + 1)
    to_right = jnp.concatenate([to_right[..., :half], to_right[..., half:] + from_left], axis=-1)
    got_right = lax.ppermute(to_left, axis, bwd)
    got_left = lax.ppermute(to_right, axis, fwd)
    return take(idx) + got_right + got_left


def shards(hidden, norm_gain, w_query, w_keyval, key_cache, value_cache, lengths, w_out):
    width_part = w_query.shape[0]
    query_cols = w_query.shape[1]
    pair_cols = w_keyval.shape[1]
    peers = 32
    values = hidden.astype(jnp.float32)
    inverse = lax.rsqrt(jnp.mean(values * values, axis=1, keepdims=True) + 1e-05)
    normed = (values * inverse * norm_gain.astype(jnp.float32)).astype(jnp.bfloat16)
    own_cols = lax.dynamic_slice_in_dim(normed, lax.axis_index("gx") * width_part, width_part, 1)
    pair = lax.all_gather(own_cols, "zh", axis=0, tiled=False)
    first = pair[..., : width_part // 2]
    second = pair[..., width_part // 2 :]
    first = ring_all_gather(first, "y", 4, 0)
    second = ring_all_gather(second, "x", 4, 0)
    first = ring_all_gather(first, "x", 4, 0)
    second = ring_all_gather(second, "y", 4, 1)
    gathered = jnp.concatenate([first, second], axis=-1).reshape(-1, width_part)
    projected = jnp.concatenate(
        [
            jnp.dot(gathered, w_query, preferred_element_type=jnp.float32),
            jnp.dot(gathered, w_keyval, preferred_element_type=jnp.float32),
        ],
        axis=1,
    )
    projected = projected.reshape(4, 4, 2, -1, projected.shape[1]).transpose(2, 0, 1, 3, 4)
    projected = projected.reshape(-1, projected.shape[-1])
    arrived = lax.all_to_all(projected.astype(jnp.bfloat16), ALL, split_axis=0, concat_axis=0, tiled=True)
    rows_dev = arrived.shape[0] // 128
    summed = arrived.reshape(4, peers, rows_dev, query_cols + pair_cols).astype(jnp.float32).sum(axis=0)
    split_cols = summed.astype(jnp.bfloat16).transpose(1, 0, 2)
    query = split_cols[:, :, :query_cols].reshape(rows_dev, peers * query_cols)
    keyval = split_cols[:, :, query_cols:].reshape(rows_dev, peers * pair_cols)
    attended = attend_rows(query, keyval, key_cache, value_cache, lengths)
    heads_first = attended.reshape(rows_dev, peers, query_cols).transpose(1, 0, 2)
    sent = jnp.broadcast_to(heads_first[None], (4,) + heads_first.shape).reshape(-1, query_cols)
    full_rows = lax.all_to_all(sent, ALL, split_axis=0, concat_axis=0, tiled=True)
    partial_out = jnp.dot(full_rows, w_out, preferred_element_type=jnp.float32)
    part = partial_out.astype(jnp.bfloat16)
    rows, cols = part.shape
    part = part.reshape(2, 4, 4, rows // peers, cols)
    first, second = part[..., : cols // 2], part[..., cols // 2 :]
    first = ring_reduce_scatter(first, "y", 2)
    second = ring_reduce_scatter(second, "x", 1)
    first = ring_reduce_scatter(first, "x", 1)
    second = ring_reduce_scatter(second, "y", 1)
    first = ring_reduce_scatter(first, "zh", 0)
    second = ring_reduce_scatter(second, "zh", 0)
    return jnp.concatenate([first, second], axis=-1)


def solution(mesh):
    from jax.sharding import Mesh
    mesh = Mesh(mesh.devices.reshape(4, 2, 4, 4), ("gx", "zh", "x", "y"))
    in_specs = (
        P(GY, None),
        P(),
        P("gx", GY),
        P("gx", GY),
        P(("gx",) + GY, None, None, None),
        P(("gx",) + GY, None, None, None),
        P(("gx",) + GY),
        P(GY, "gx"),
    )
    out_specs = P(GY, "gx")
    return jax.shard_map(shards, mesh=mesh, in_specs=in_specs, out_specs=out_specs, check_vma=False)
```

```python
import math

import jax
import jax.numpy as jnp
from jax import lax
from jax.sharding import PartitionSpec as P

GY = ("zh", "x", "y")
ALL = ("gx",) + GY


def rotate_heads(values, position, head_dim):
    half = head_dim // 2
    freq = jnp.exp(-(jnp.arange(half, dtype=jnp.float32) * 2.0 / head_dim) * math.log(500000.0))
    angle = position[:, None] * freq[None, :]
    cosine = jnp.cos(angle)[:, None, :]
    sine = jnp.sin(angle)[:, None, :]
    first = values[..., :half]
    second = values[..., half:]
    return jnp.concatenate(
        [first * cosine - second * sine, second * cosine + first * sine], axis=-1
    )


def attend_rows(query, keyval, key_cache, value_cache, lengths):
    rows, cache_len, kv_heads, head_dim = key_cache.shape
    heads = query.shape[1] // head_dim
    group = heads // kv_heads
    scale = 1.0 / math.sqrt(head_dim)
    position = lengths.astype(jnp.float32)
    rotated = rotate_heads(
        query.astype(jnp.float32).reshape(rows, heads, head_dim), position, head_dim
    ).astype(jnp.bfloat16)
    pairs = keyval.reshape(rows, 2, kv_heads, head_dim)
    new_key = rotate_heads(pairs[:, 0].astype(jnp.float32), position, head_dim).astype(jnp.bfloat16)
    new_value = pairs[:, 1].astype(jnp.float32)
    grouped = rotated.reshape(rows, kv_heads, group, head_dim)
    scores = (
        jnp.einsum("rgqd,rtgd->rgqt", grouped, key_cache, preferred_element_type=jnp.float32)
        * scale
    )
    own = jnp.einsum("rgqd,rgd->rgq", grouped, new_key, preferred_element_type=jnp.float32) * scale
    valid = jnp.arange(cache_len)[None, None, None, :] < lengths[:, None, None, None]
    scores = jnp.where(valid, scores, -jnp.inf)
    top = jnp.maximum(jnp.max(scores, axis=-1), own)
    weights = jnp.exp(scores - top[..., None])
    own_weight = jnp.exp(own - top)
    total = jnp.sum(weights, axis=-1) + own_weight
    probs = (weights / total[..., None]).astype(jnp.bfloat16)
    own_prob = (own_weight / total).astype(jnp.bfloat16)
    result = jnp.einsum("rgqt,rtgd->rgqd", probs, value_cache, preferred_element_type=jnp.float32)
    result = result + own_prob.astype(jnp.float32)[..., None] * new_value[:, :, None, :]
    return result.astype(jnp.bfloat16).reshape(rows, heads * head_dim)


def ring_all_gather(blk, axis, n, dim):
    idx = lax.axis_index(axis)
    fwd = [(i, (i + 1) % n) for i in range(n)]
    bwd = [(i, (i - 1) % n) for i in range(n)]
    out = jnp.zeros(blk.shape[:dim] + (n,) + blk.shape[dim:], blk.dtype)
    out = lax.dynamic_update_index_in_dim(out, blk, idx, dim)
    from_left = lax.ppermute(blk, axis, fwd)
    out = lax.dynamic_update_index_in_dim(out, from_left, (idx - 1) % n, dim)
    if n == 2:
        return out
    from_right = lax.ppermute(blk, axis, bwd)
    out = lax.dynamic_update_index_in_dim(out, from_right, (idx + 1) % n, dim)
    half = blk.shape[-1] // 2
    first = lax.ppermute(from_left[..., :half], axis, fwd)
    second = lax.ppermute(from_right[..., half:], axis, bwd)
    opposite = jnp.concatenate([first, second], axis=-1)
    return lax.dynamic_update_index_in_dim(out, opposite, (idx + 2) % n, dim)


def ring_all_gather_apply(blk, axis, n, dim, fn):
    idx = lax.axis_index(axis)
    fwd = [(i, (i + 1) % n) for i in range(n)]
    bwd = [(i, (i - 1) % n) for i in range(n)]
    from_left = lax.ppermute(blk, axis, fwd)
    from_right = lax.ppermute(blk, axis, bwd)
    own = fn(blk)
    out = jnp.zeros(own.shape[:dim] + (n,) + own.shape[dim:], own.dtype)
    out = lax.dynamic_update_index_in_dim(out, own, idx, dim)
    half = blk.shape[-1] // 2
    first = lax.ppermute(from_left[..., :half], axis, fwd)
    second = lax.ppermute(from_right[..., half:], axis, bwd)
    out = lax.dynamic_update_index_in_dim(out, fn(from_left), (idx - 1) % n, dim)
    out = lax.dynamic_update_index_in_dim(out, fn(from_right), (idx + 1) % n, dim)
    opposite = jnp.concatenate([first, second], axis=-1)
    return lax.dynamic_update_index_in_dim(out, fn(opposite), (idx + 2) % n, dim)


def blocks_of(arr, dim):
    return lambda k: lax.dynamic_index_in_dim(arr, k, dim, keepdims=False)


def ring_reduce_scatter(make, axis, n):
    idx = lax.axis_index(axis)

    def take(k):
        return make(k % n)

    fwd = [(i, (i + 1) % n) for i in range(n)]
    bwd = [(i, (i - 1) % n) for i in range(n)]
    if n == 2:
        return take(idx) + lax.ppermute(take(idx + 1), axis, fwd)
    opposite = take(idx + 2)
    half = opposite.shape[-1] // 2
    from_right = lax.ppermute(opposite[..., :half], axis, bwd)
    from_left = lax.ppermute(opposite[..., half:], axis, fwd)
    to_left = take(idx - 1)
    to_left = jnp.concatenate([to_left[..., :half] + from_right, to_left[..., half:]], axis=-1)
    to_right = take(idx + 1)
    to_right = jnp.concatenate([to_right[..., :half], to_right[..., half:] + from_left], axis=-1)
    got_right = lax.ppermute(to_left, axis, bwd)
    got_left = lax.ppermute(to_right, axis, fwd)
    return take(idx) + got_right + got_left


def shards(hidden, norm_gain, w_query, w_keyval, key_cache, value_cache, lengths, w_out):
    width_part = w_query.shape[0]
    query_cols = w_query.shape[1]
    pair_cols = w_keyval.shape[1]
    peers = 32
    values = hidden.astype(jnp.float32)
    inverse = lax.rsqrt(jnp.mean(values * values, axis=1, keepdims=True) + 1e-05)
    normed = (values * inverse * norm_gain.astype(jnp.float32)).astype(jnp.bfloat16)
    own_cols = lax.dynamic_slice_in_dim(normed, lax.axis_index("gx") * width_part, width_part, 1)
    pair = lax.all_gather(own_cols, "zh", axis=0, tiled=False)
    first = pair[..., : width_part // 2]
    second = pair[..., width_part // 2 :]
    first = ring_all_gather(first, "y", 4, 0)
    second = ring_all_gather(second, "x", 4, 0)
    half = width_part // 2

    def project(lo, hi):
        return lambda piece: jnp.concatenate(
            [
                jnp.dot(piece, w_query[lo:hi], preferred_element_type=jnp.float32),
                jnp.dot(piece, w_keyval[lo:hi], preferred_element_type=jnp.float32),
            ],
            axis=-1,
        )

    projected = ring_all_gather_apply(first, "x", 4, 0, project(0, half))
    projected = projected + ring_all_gather_apply(second, "y", 4, 1, project(half, width_part))
    projected = projected.reshape(-1, query_cols + pair_cols)
    projected = projected.reshape(4, 4, 2, -1, projected.shape[1]).transpose(2, 0, 1, 3, 4)
    projected = projected.reshape(-1, projected.shape[-1])
    arrived = lax.all_to_all(projected.astype(jnp.bfloat16), ALL, split_axis=0, concat_axis=0, tiled=True)
    rows_dev = arrived.shape[0] // 128
    summed = arrived.reshape(4, peers, rows_dev, query_cols + pair_cols).astype(jnp.float32).sum(axis=0)
    split_cols = summed.astype(jnp.bfloat16).transpose(1, 0, 2)
    query = split_cols[:, :, :query_cols].reshape(rows_dev, peers * query_cols)
    keyval = split_cols[:, :, query_cols:].reshape(rows_dev, peers * pair_cols)
    attended = attend_rows(query, keyval, key_cache, value_cache, lengths)
    heads_first = attended.reshape(rows_dev, peers, query_cols).transpose(1, 0, 2)
    sent = jnp.broadcast_to(heads_first[None], (4,) + heads_first.shape).reshape(-1, query_cols)
    full_rows = lax.all_to_all(sent, ALL, split_axis=0, concat_axis=0, tiled=True)
    cols = w_out.shape[1]
    by_row = full_rows.reshape(2, 4, 4, rows_dev * 4, query_cols)

    def partial_out(dim, lo, hi):
        return lambda k: jnp.dot(
            lax.dynamic_index_in_dim(by_row, k, dim, keepdims=False),
            w_out[:, lo:hi],
            preferred_element_type=jnp.float32,
        ).astype(jnp.bfloat16)

    first = ring_reduce_scatter(partial_out(2, 0, cols // 2), "y", 4)
    second = ring_reduce_scatter(partial_out(1, cols // 2, cols), "x", 4)
    first = ring_reduce_scatter(blocks_of(first, 1), "x", 4)
    second = ring_reduce_scatter(blocks_of(second, 1), "y", 4)
    first = ring_reduce_scatter(blocks_of(first, 0), "zh", 2)
    second = ring_reduce_scatter(blocks_of(second, 0), "zh", 2)
    return jnp.concatenate([first, second], axis=-1)


def solution(mesh):
    from jax.sharding import Mesh
    mesh = Mesh(mesh.devices.reshape(4, 2, 4, 4), ("gx", "zh", "x", "y"))
    in_specs = (
        P(GY, None),
        P(),
        P("gx", GY),
        P("gx", GY),
        P(("gx",) + GY, None, None, None),
        P(("gx",) + GY, None, None, None),
        P(("gx",) + GY),
        P(GY, "gx"),
    )
    out_specs = P(GY, "gx")
    return jax.shard_map(shards, mesh=mesh, in_specs=in_specs, out_specs=out_specs, check_vma=False)
```

```python
import math

import jax
import jax.numpy as jnp
from jax import lax
from jax.sharding import PartitionSpec as P

GY = ("zh", "x", "y")
ALL = ("gx",) + GY


def rotate_heads(values, position, head_dim):
    half = head_dim // 2
    freq = jnp.exp(-(jnp.arange(half, dtype=jnp.float32) * 2.0 / head_dim) * math.log(500000.0))
    angle = position[:, None] * freq[None, :]
    cosine = jnp.cos(angle)[:, None, :]
    sine = jnp.sin(angle)[:, None, :]
    first = values[..., :half]
    second = values[..., half:]
    return jnp.concatenate(
        [first * cosine - second * sine, second * cosine + first * sine], axis=-1
    )


def attend_rows(query, keyval, key_cache, value_cache, lengths):
    rows, cache_len, kv_heads, head_dim = key_cache.shape
    heads = query.shape[1] // head_dim
    group = heads // kv_heads
    scale = 1.0 / math.sqrt(head_dim)
    position = lengths.astype(jnp.float32)
    rotated = rotate_heads(
        query.astype(jnp.float32).reshape(rows, heads, head_dim), position, head_dim
    ).astype(jnp.bfloat16)
    pairs = keyval.reshape(rows, 2, kv_heads, head_dim)
    new_key = rotate_heads(pairs[:, 0].astype(jnp.float32), position, head_dim).astype(jnp.bfloat16)
    new_value = pairs[:, 1].astype(jnp.float32)
    grouped = rotated.reshape(rows, kv_heads, group, head_dim)
    scores = (
        jnp.einsum("rgqd,rtgd->rgqt", grouped, key_cache, preferred_element_type=jnp.float32)
        * scale
    )
    own = jnp.einsum("rgqd,rgd->rgq", grouped, new_key, preferred_element_type=jnp.float32) * scale
    valid = jnp.arange(cache_len)[None, None, None, :] < lengths[:, None, None, None]
    scores = jnp.where(valid, scores, -jnp.inf)
    top = jnp.maximum(jnp.max(scores, axis=-1), own)
    weights = jnp.exp(scores - top[..., None])
    own_weight = jnp.exp(own - top)
    total = jnp.sum(weights, axis=-1) + own_weight
    probs = (weights / total[..., None]).astype(jnp.bfloat16)
    own_prob = (own_weight / total).astype(jnp.bfloat16)
    result = jnp.einsum("rgqt,rtgd->rgqd", probs, value_cache, preferred_element_type=jnp.float32)
    result = result + own_prob.astype(jnp.float32)[..., None] * new_value[:, :, None, :]
    return result.astype(jnp.bfloat16).reshape(rows, heads * head_dim)


def ring_all_gather(blk, axis, n, dim):
    idx = lax.axis_index(axis)
    fwd = [(i, (i + 1) % n) for i in range(n)]
    bwd = [(i, (i - 1) % n) for i in range(n)]
    out = jnp.zeros(blk.shape[:dim] + (n,) + blk.shape[dim:], blk.dtype)
    out = lax.dynamic_update_index_in_dim(out, blk, idx, dim)
    from_left = lax.ppermute(blk, axis, fwd)
    out = lax.dynamic_update_index_in_dim(out, from_left, (idx - 1) % n, dim)
    if n == 2:
        return out
    from_right = lax.ppermute(blk, axis, bwd)
    out = lax.dynamic_update_index_in_dim(out, from_right, (idx + 1) % n, dim)
    half = blk.shape[-1] // 2
    first = lax.ppermute(from_left[..., :half], axis, fwd)
    second = lax.ppermute(from_right[..., half:], axis, bwd)
    opposite = jnp.concatenate([first, second], axis=-1)
    return lax.dynamic_update_index_in_dim(out, opposite, (idx + 2) % n, dim)


def ring_all_gather_apply(blk, axis, n, dim, fn):
    idx = lax.axis_index(axis)
    fwd = [(i, (i + 1) % n) for i in range(n)]
    bwd = [(i, (i - 1) % n) for i in range(n)]
    from_left = lax.ppermute(blk, axis, fwd)
    from_right = lax.ppermute(blk, axis, bwd)
    own = fn(blk)
    out = jnp.zeros(own.shape[:dim] + (n,) + own.shape[dim:], own.dtype)
    out = lax.dynamic_update_index_in_dim(out, own, idx, dim)
    half = blk.shape[-1] // 2
    first = lax.ppermute(from_left[..., :half], axis, fwd)
    second = lax.ppermute(from_right[..., half:], axis, bwd)
    out = lax.dynamic_update_index_in_dim(out, fn(from_left), (idx - 1) % n, dim)
    out = lax.dynamic_update_index_in_dim(out, fn(from_right), (idx + 1) % n, dim)
    opposite = jnp.concatenate([first, second], axis=-1)
    return lax.dynamic_update_index_in_dim(out, fn(opposite), (idx + 2) % n, dim)


def blocks_of(arr, dim):
    return lambda k: lax.dynamic_index_in_dim(arr, k, dim, keepdims=False)


def ring_reduce_scatter(make, axis, n):
    idx = lax.axis_index(axis)

    def take(k):
        return make(k % n)

    fwd = [(i, (i + 1) % n) for i in range(n)]
    bwd = [(i, (i - 1) % n) for i in range(n)]
    if n == 2:
        return take(idx) + lax.ppermute(take(idx + 1), axis, fwd)
    opposite = take(idx + 2)
    half = opposite.shape[-1] // 2
    from_right = lax.ppermute(opposite[..., :half], axis, bwd)
    from_left = lax.ppermute(opposite[..., half:], axis, fwd)
    to_left = take(idx - 1)
    to_left = jnp.concatenate([to_left[..., :half] + from_right, to_left[..., half:]], axis=-1)
    to_right = take(idx + 1)
    to_right = jnp.concatenate([to_right[..., :half], to_right[..., half:] + from_left], axis=-1)
    got_right = lax.ppermute(to_left, axis, bwd)
    got_left = lax.ppermute(to_right, axis, fwd)
    return take(idx) + got_right + got_left


def neighbour_pairs():
    pairs = []
    for gx in range(4):
        for gy in range(32):
            pairs.append((gx * 32 + gy, ((gx + 2) % 4) * 32 + (gy + 16) % 32))
    return pairs


def shards(hidden, norm_gain, w_query, w_keyval, key_cache, value_cache, lengths, w_out):
    width_part = w_query.shape[0]
    query_cols = w_query.shape[1]
    pair_cols = w_keyval.shape[1]
    peers = 32
    values = hidden.astype(jnp.float32)
    inverse = lax.rsqrt(jnp.mean(values * values, axis=1, keepdims=True) + 1e-05)
    normed = (values * inverse * norm_gain.astype(jnp.float32)).astype(jnp.bfloat16)
    gx = lax.axis_index("gx")
    own_cols = lax.dynamic_slice_in_dim(normed, gx * width_part, width_part, 1)
    partner_gx = (gx + 2) % 4
    sent = lax.dynamic_slice_in_dim(normed, partner_gx * width_part, width_part, 1)
    got = lax.ppermute(sent, ALL, neighbour_pairs())
    zh = lax.axis_index("zh")
    pair = jnp.zeros((2,) + own_cols.shape, own_cols.dtype)
    pair = lax.dynamic_update_index_in_dim(pair, own_cols, zh, 0)
    pair = lax.dynamic_update_index_in_dim(pair, got, 1 - zh, 0)
    first = pair[..., : width_part // 2]
    second = pair[..., width_part // 2 :]
    first = ring_all_gather(first, "y", 4, 0)
    second = ring_all_gather(second, "x", 4, 0)
    half = width_part // 2

    def project(lo, hi):
        return lambda piece: jnp.concatenate(
            [
                jnp.dot(piece, w_query[lo:hi], preferred_element_type=jnp.float32),
                jnp.dot(piece, w_keyval[lo:hi], preferred_element_type=jnp.float32),
            ],
            axis=-1,
        )

    projected = ring_all_gather_apply(first, "x", 4, 0, project(0, half))
    projected = projected + ring_all_gather_apply(second, "y", 4, 1, project(half, width_part))
    projected = projected.reshape(-1, query_cols + pair_cols)
    projected = projected.reshape(4, 4, 2, -1, projected.shape[1]).transpose(2, 0, 1, 3, 4)
    projected = projected.reshape(-1, projected.shape[-1])
    arrived = lax.all_to_all(projected.astype(jnp.bfloat16), ALL, split_axis=0, concat_axis=0, tiled=True)
    rows_dev = arrived.shape[0] // 128
    summed = arrived.reshape(4, peers, rows_dev, query_cols + pair_cols).astype(jnp.float32).sum(axis=0)
    split_cols = summed.astype(jnp.bfloat16).transpose(1, 0, 2)
    query = split_cols[:, :, :query_cols].reshape(rows_dev, peers * query_cols)
    keyval = split_cols[:, :, query_cols:].reshape(rows_dev, peers * pair_cols)
    attended = attend_rows(query, keyval, key_cache, value_cache, lengths)
    heads_first = attended.reshape(rows_dev, peers, query_cols).transpose(1, 0, 2)
    sent = jnp.broadcast_to(heads_first[None], (4,) + heads_first.shape).reshape(-1, query_cols)
    full_rows = lax.all_to_all(sent, ALL, split_axis=0, concat_axis=0, tiled=True)
    cols = w_out.shape[1]
    by_row = full_rows.reshape(2, 4, 4, rows_dev * 4, query_cols)

    def partial_out(dim, lo, hi):
        return lambda k: jnp.dot(
            lax.dynamic_index_in_dim(by_row, k, dim, keepdims=False),
            w_out[:, lo:hi],
            preferred_element_type=jnp.float32,
        ).astype(jnp.bfloat16)

    first = ring_reduce_scatter(partial_out(2, 0, cols // 2), "y", 4)
    second = ring_reduce_scatter(partial_out(1, cols // 2, cols), "x", 4)
    first = ring_reduce_scatter(blocks_of(first, 1), "x", 4)
    second = ring_reduce_scatter(blocks_of(second, 1), "y", 4)
    first = ring_reduce_scatter(blocks_of(first, 0), "zh", 2)
    second = ring_reduce_scatter(blocks_of(second, 0), "zh", 2)
    return jnp.concatenate([first, second], axis=-1)


def solution(mesh):
    from jax.sharding import Mesh
    mesh = Mesh(mesh.devices.reshape(4, 2, 4, 4), ("gx", "zh", "x", "y"))
    in_specs = (
        P(GY, None),
        P(),
        P("gx", GY),
        P("gx", GY),
        P(("gx",) + GY, None, None, None),
        P(("gx",) + GY, None, None, None),
        P(("gx",) + GY),
        P(GY, "gx"),
    )
    out_specs = P(GY, "gx")
    return jax.shard_map(shards, mesh=mesh, in_specs=in_specs, out_specs=out_specs, check_vma=False)
```

```python
import math

import jax
import jax.numpy as jnp
from jax import lax
from jax.sharding import PartitionSpec as P

GY = ("zh", "x", "y")
ALL = ("gx",) + GY


def rotate_heads(values, position, head_dim):
    half = head_dim // 2
    freq = jnp.exp(-(jnp.arange(half, dtype=jnp.float32) * 2.0 / head_dim) * math.log(500000.0))
    angle = position[:, None] * freq[None, :]
    cosine = jnp.cos(angle)[:, None, :]
    sine = jnp.sin(angle)[:, None, :]
    first = values[..., :half]
    second = values[..., half:]
    return jnp.concatenate(
        [first * cosine - second * sine, second * cosine + first * sine], axis=-1
    )


def attend_rows(query, keyval, key_cache, value_cache, lengths):
    rows, cache_len, kv_heads, head_dim = key_cache.shape
    heads = query.shape[1] // head_dim
    group = heads // kv_heads
    scale = 1.0 / math.sqrt(head_dim)
    position = lengths.astype(jnp.float32)
    rotated = rotate_heads(
        query.astype(jnp.float32).reshape(rows, heads, head_dim), position, head_dim
    ).astype(jnp.bfloat16)
    pairs = keyval.reshape(rows, 2, kv_heads, head_dim)
    new_key = rotate_heads(pairs[:, 0].astype(jnp.float32), position, head_dim).astype(jnp.bfloat16)
    new_value = pairs[:, 1].astype(jnp.float32)
    grouped = rotated.reshape(rows, kv_heads, group, head_dim)
    scores = (
        jnp.einsum("rgqd,rtgd->rgqt", grouped, key_cache, preferred_element_type=jnp.float32)
        * scale
    )
    own = jnp.einsum("rgqd,rgd->rgq", grouped, new_key, preferred_element_type=jnp.float32) * scale
    valid = jnp.arange(cache_len)[None, None, None, :] < lengths[:, None, None, None]
    scores = jnp.where(valid, scores, -jnp.inf)
    top = jnp.maximum(jnp.max(scores, axis=-1), own)
    weights = jnp.exp(scores - top[..., None])
    own_weight = jnp.exp(own - top)
    total = jnp.sum(weights, axis=-1) + own_weight
    probs = (weights / total[..., None]).astype(jnp.bfloat16)
    own_prob = (own_weight / total).astype(jnp.bfloat16)
    result = jnp.einsum("rgqt,rtgd->rgqd", probs, value_cache, preferred_element_type=jnp.float32)
    result = result + own_prob.astype(jnp.float32)[..., None] * new_value[:, :, None, :]
    return result.astype(jnp.bfloat16).reshape(rows, heads * head_dim)


def ring_all_gather(blk, axis, n, dim):
    idx = lax.axis_index(axis)
    fwd = [(i, (i + 1) % n) for i in range(n)]
    bwd = [(i, (i - 1) % n) for i in range(n)]
    out = jnp.zeros(blk.shape[:dim] + (n,) + blk.shape[dim:], blk.dtype)
    out = lax.dynamic_update_index_in_dim(out, blk, idx, dim)
    from_left = lax.ppermute(blk, axis, fwd)
    out = lax.dynamic_update_index_in_dim(out, from_left, (idx - 1) % n, dim)
    if n == 2:
        return out
    from_right = lax.ppermute(blk, axis, bwd)
    out = lax.dynamic_update_index_in_dim(out, from_right, (idx + 1) % n, dim)
    half = blk.shape[-1] // 2
    first = lax.ppermute(from_left[..., :half], axis, fwd)
    second = lax.ppermute(from_right[..., half:], axis, bwd)
    opposite = jnp.concatenate([first, second], axis=-1)
    return lax.dynamic_update_index_in_dim(out, opposite, (idx + 2) % n, dim)


def ring_all_gather_apply(blk, axis, n, dim, fn):
    idx = lax.axis_index(axis)
    fwd = [(i, (i + 1) % n) for i in range(n)]
    bwd = [(i, (i - 1) % n) for i in range(n)]
    from_left = lax.ppermute(blk, axis, fwd)
    from_right = lax.ppermute(blk, axis, bwd)
    own = fn(blk)
    out = jnp.zeros(own.shape[:dim] + (n,) + own.shape[dim:], own.dtype)
    out = lax.dynamic_update_index_in_dim(out, own, idx, dim)
    half = blk.shape[-1] // 2
    first = lax.ppermute(from_left[..., :half], axis, fwd)
    second = lax.ppermute(from_right[..., half:], axis, bwd)
    out = lax.dynamic_update_index_in_dim(out, fn(from_left), (idx - 1) % n, dim)
    out = lax.dynamic_update_index_in_dim(out, fn(from_right), (idx + 1) % n, dim)
    opposite = jnp.concatenate([first, second], axis=-1)
    return lax.dynamic_update_index_in_dim(out, fn(opposite), (idx + 2) % n, dim)


def blocks_of(arr, dim):
    return lambda k: lax.dynamic_index_in_dim(arr, k, dim, keepdims=False)


def ring_reduce_scatter(make, axis, n):
    idx = lax.axis_index(axis)

    def take(k):
        return make(k % n)

    fwd = [(i, (i + 1) % n) for i in range(n)]
    bwd = [(i, (i - 1) % n) for i in range(n)]
    if n == 2:
        return take(idx) + lax.ppermute(take(idx + 1), axis, fwd)
    opposite = take(idx + 2)
    half = opposite.shape[-1] // 2
    from_right = lax.ppermute(opposite[..., :half], axis, bwd)
    from_left = lax.ppermute(opposite[..., half:], axis, fwd)
    to_left = take(idx - 1)
    to_left = jnp.concatenate([to_left[..., :half] + from_right, to_left[..., half:]], axis=-1)
    to_right = take(idx + 1)
    to_right = jnp.concatenate([to_right[..., :half], to_right[..., half:] + from_left], axis=-1)
    got_right = lax.ppermute(to_left, axis, bwd)
    got_left = lax.ppermute(to_right, axis, fwd)
    return take(idx) + got_right + got_left


def neighbour_pairs():
    pairs = []
    for gx in range(4):
        for gy in range(32):
            pairs.append((gx * 32 + gy, ((gx + 2) % 4) * 32 + (gy + 16) % 32))
    return pairs


def shards(hidden, norm_gain, w_query, w_keyval, key_cache, value_cache, lengths, w_out):
    width_part = w_query.shape[0]
    query_cols = w_query.shape[1]
    pair_cols = w_keyval.shape[1]
    peers = 32
    values = hidden.astype(jnp.float32)
    inverse = lax.rsqrt(jnp.mean(values * values, axis=1, keepdims=True) + 1e-05)
    normed = (values * inverse * norm_gain.astype(jnp.float32)).astype(jnp.bfloat16)
    gx = lax.axis_index("gx")
    own_cols = lax.dynamic_slice_in_dim(normed, gx * width_part, width_part, 1)
    partner_gx = (gx + 2) % 4
    sent = lax.dynamic_slice_in_dim(normed, partner_gx * width_part, width_part, 1)
    got = lax.ppermute(sent, ALL, neighbour_pairs())
    zh = lax.axis_index("zh")
    pair = jnp.zeros((2,) + own_cols.shape, own_cols.dtype)
    pair = lax.dynamic_update_index_in_dim(pair, own_cols, zh, 0)
    pair = lax.dynamic_update_index_in_dim(pair, got, 1 - zh, 0)
    first = pair[..., : width_part // 2]
    second = pair[..., width_part // 2 :]
    first = ring_all_gather(first, "y", 4, 0)
    second = ring_all_gather(second, "x", 4, 0)
    half = width_part // 2

    def project(lo, hi):
        return lambda piece: jnp.concatenate(
            [
                jnp.dot(piece, w_query[lo:hi], preferred_element_type=jnp.float32),
                jnp.dot(piece, w_keyval[lo:hi], preferred_element_type=jnp.float32),
            ],
            axis=-1,
        )

    projected = ring_all_gather_apply(first, "x", 4, 0, project(0, half))
    projected = projected + ring_all_gather_apply(second, "y", 4, 1, project(half, width_part))
    projected = projected.reshape(-1, query_cols + pair_cols)
    projected = projected.reshape(4, 4, 2, -1, projected.shape[1]).transpose(2, 0, 1, 3, 4)
    projected = projected.reshape(-1, projected.shape[-1])
    arrived = lax.all_to_all(projected.astype(jnp.bfloat16), ALL, split_axis=0, concat_axis=0, tiled=True)
    rows_dev = arrived.shape[0] // 128
    summed = arrived.reshape(4, peers, rows_dev, query_cols + pair_cols).astype(jnp.float32).sum(axis=0)
    split_cols = summed.astype(jnp.bfloat16).transpose(1, 0, 2)
    query = split_cols[:, :, :query_cols].reshape(rows_dev, peers * query_cols)
    keyval = split_cols[:, :, query_cols:].reshape(rows_dev, peers * pair_cols)
    attended = attend_rows(query, keyval, key_cache, value_cache, lengths)
    heads_first = attended.reshape(rows_dev, peers, query_cols).transpose(1, 0, 2)
    sent = jnp.broadcast_to(heads_first[None], (4,) + heads_first.shape).reshape(-1, query_cols)
    full_rows = lax.all_to_all(sent, ALL, split_axis=0, concat_axis=0, tiled=True)
    cols = w_out.shape[1]
    by_row = full_rows.reshape(2, 4, 4, rows_dev * 4, query_cols)

    def partial_out(dim, lo, hi):
        return lambda k: jnp.dot(
            lax.dynamic_index_in_dim(by_row, k, dim, keepdims=False),
            w_out[:, lo:hi],
            preferred_element_type=jnp.float32,
        ).astype(jnp.bfloat16)

    first = ring_reduce_scatter(partial_out(2, 0, cols // 2), "y", 4)
    second = ring_reduce_scatter(partial_out(1, cols // 2, cols), "x", 4)
    first = lax.all_to_all(first.reshape((8,) + first.shape[2:]), ("zh", "x"), 0, 0, tiled=True)
    second = lax.all_to_all(second.reshape((8,) + second.shape[2:]), ("zh", "y"), 0, 0, tiled=True)
    first = first.astype(jnp.float32).sum(axis=0)
    second = second.astype(jnp.float32).sum(axis=0)
    return jnp.concatenate([first, second], axis=-1).astype(jnp.bfloat16)


def solution(mesh):
    from jax.sharding import Mesh
    mesh = Mesh(mesh.devices.reshape(4, 2, 4, 4), ("gx", "zh", "x", "y"))
    in_specs = (
        P(GY, None),
        P(),
        P("gx", GY),
        P("gx", GY),
        P(("gx",) + GY, None, None, None),
        P(("gx",) + GY, None, None, None),
        P(("gx",) + GY),
        P(GY, "gx"),
    )
    out_specs = P(GY, "gx")
    return jax.shard_map(shards, mesh=mesh, in_specs=in_specs, out_specs=out_specs, check_vma=False)
```

```python
import math

import jax
import jax.numpy as jnp
from jax import lax
from jax.sharding import PartitionSpec as P

GY = ("zh", "x", "y")
ALL = ("gx",) + GY


def rotate_heads(values, position, head_dim):
    half = head_dim // 2
    freq = jnp.exp(-(jnp.arange(half, dtype=jnp.float32) * 2.0 / head_dim) * math.log(500000.0))
    angle = position[:, None] * freq[None, :]
    cosine = jnp.cos(angle)[:, None, :]
    sine = jnp.sin(angle)[:, None, :]
    first = values[..., :half]
    second = values[..., half:]
    return jnp.concatenate(
        [first * cosine - second * sine, second * cosine + first * sine], axis=-1
    )


def attend_rows(query, keyval, key_cache, value_cache, lengths):
    rows, cache_len, kv_heads, head_dim = key_cache.shape
    heads = query.shape[1] // head_dim
    group = heads // kv_heads
    scale = 1.0 / math.sqrt(head_dim)
    position = lengths.astype(jnp.float32)
    rotated = rotate_heads(
        query.astype(jnp.float32).reshape(rows, heads, head_dim), position, head_dim
    ).astype(jnp.bfloat16)
    pairs = keyval.reshape(rows, 2, kv_heads, head_dim)
    new_key = rotate_heads(pairs[:, 0].astype(jnp.float32), position, head_dim).astype(jnp.bfloat16)
    new_value = pairs[:, 1].astype(jnp.float32)
    grouped = rotated.reshape(rows, kv_heads, group, head_dim)
    scores = (
        jnp.einsum("rgqd,rtgd->rgqt", grouped, key_cache, preferred_element_type=jnp.float32)
        * scale
    )
    own = jnp.einsum("rgqd,rgd->rgq", grouped, new_key, preferred_element_type=jnp.float32) * scale
    valid = jnp.arange(cache_len)[None, None, None, :] < lengths[:, None, None, None]
    scores = jnp.where(valid, scores, -jnp.inf)
    top = jnp.maximum(jnp.max(scores, axis=-1), own)
    weights = jnp.exp(scores - top[..., None])
    own_weight = jnp.exp(own - top)
    total = jnp.sum(weights, axis=-1) + own_weight
    probs = (weights / total[..., None]).astype(jnp.bfloat16)
    own_prob = (own_weight / total).astype(jnp.bfloat16)
    result = jnp.einsum("rgqt,rtgd->rgqd", probs, value_cache, preferred_element_type=jnp.float32)
    result = result + own_prob.astype(jnp.float32)[..., None] * new_value[:, :, None, :]
    return result.astype(jnp.bfloat16).reshape(rows, heads * head_dim)


def ring_all_gather(blk, axis, n, dim):
    idx = lax.axis_index(axis)
    fwd = [(i, (i + 1) % n) for i in range(n)]
    bwd = [(i, (i - 1) % n) for i in range(n)]
    out = jnp.zeros(blk.shape[:dim] + (n,) + blk.shape[dim:], blk.dtype)
    out = lax.dynamic_update_index_in_dim(out, blk, idx, dim)
    from_left = lax.ppermute(blk, axis, fwd)
    out = lax.dynamic_update_index_in_dim(out, from_left, (idx - 1) % n, dim)
    if n == 2:
        return out
    from_right = lax.ppermute(blk, axis, bwd)
    out = lax.dynamic_update_index_in_dim(out, from_right, (idx + 1) % n, dim)
    half = blk.shape[-1] // 2
    first = lax.ppermute(from_left[..., :half], axis, fwd)
    second = lax.ppermute(from_right[..., half:], axis, bwd)
    opposite = jnp.concatenate([first, second], axis=-1)
    return lax.dynamic_update_index_in_dim(out, opposite, (idx + 2) % n, dim)


def direct_all_gather(blk, axis, n, dim):
    idx = lax.axis_index(axis)
    out = jnp.zeros(blk.shape[:dim] + (n,) + blk.shape[dim:], blk.dtype)
    out = lax.dynamic_update_index_in_dim(out, blk, idx, dim)
    for d in range(1, n):
        got = lax.ppermute(blk, axis, [(i, (i + d) % n) for i in range(n)])
        out = lax.dynamic_update_index_in_dim(out, got, (idx - d) % n, dim)
    return out


def direct_reduce_scatter(make, axis, n):
    idx = lax.axis_index(axis)
    total = make(idx).astype(jnp.float32)
    for d in range(1, n):
        got = lax.ppermute(make((idx + d) % n), axis, [(i, (i + d) % n) for i in range(n)])
        total = total + got.astype(jnp.float32)
    return total.astype(jnp.bfloat16)


def ring_all_gather_apply(blk, axis, n, dim, fn):
    idx = lax.axis_index(axis)
    fwd = [(i, (i + 1) % n) for i in range(n)]
    bwd = [(i, (i - 1) % n) for i in range(n)]
    from_left = lax.ppermute(blk, axis, fwd)
    from_right = lax.ppermute(blk, axis, bwd)
    own = fn(blk)
    out = jnp.zeros(own.shape[:dim] + (n,) + own.shape[dim:], own.dtype)
    out = lax.dynamic_update_index_in_dim(out, own, idx, dim)
    half = blk.shape[-1] // 2
    first = lax.ppermute(from_left[..., :half], axis, fwd)
    second = lax.ppermute(from_right[..., half:], axis, bwd)
    out = lax.dynamic_update_index_in_dim(out, fn(from_left), (idx - 1) % n, dim)
    out = lax.dynamic_update_index_in_dim(out, fn(from_right), (idx + 1) % n, dim)
    opposite = jnp.concatenate([first, second], axis=-1)
    return lax.dynamic_update_index_in_dim(out, fn(opposite), (idx + 2) % n, dim)


def blocks_of(arr, dim):
    return lambda k: lax.dynamic_index_in_dim(arr, k, dim, keepdims=False)


def ring_reduce_scatter(make, axis, n):
    idx = lax.axis_index(axis)

    def take(k):
        return make(k % n)

    fwd = [(i, (i + 1) % n) for i in range(n)]
    bwd = [(i, (i - 1) % n) for i in range(n)]
    if n == 2:
        return take(idx) + lax.ppermute(take(idx + 1), axis, fwd)
    opposite = take(idx + 2)
    half = opposite.shape[-1] // 2
    from_right = lax.ppermute(opposite[..., :half], axis, bwd)
    from_left = lax.ppermute(opposite[..., half:], axis, fwd)
    to_left = take(idx - 1)
    to_left = jnp.concatenate([to_left[..., :half] + from_right, to_left[..., half:]], axis=-1)
    to_right = take(idx + 1)
    to_right = jnp.concatenate([to_right[..., :half], to_right[..., half:] + from_left], axis=-1)
    got_right = lax.ppermute(to_left, axis, bwd)
    got_left = lax.ppermute(to_right, axis, fwd)
    return take(idx) + got_right + got_left


def neighbour_pairs():
    pairs = []
    for gx in range(4):
        for gy in range(32):
            pairs.append((gx * 32 + gy, ((gx + 2) % 4) * 32 + (gy + 16) % 32))
    return pairs


def shards(hidden, norm_gain, w_query, w_keyval, key_cache, value_cache, lengths, w_out):
    width_part = w_query.shape[0]
    query_cols = w_query.shape[1]
    pair_cols = w_keyval.shape[1]
    peers = 32
    values = hidden.astype(jnp.float32)
    inverse = lax.rsqrt(jnp.mean(values * values, axis=1, keepdims=True) + 1e-05)
    normed = (values * inverse * norm_gain.astype(jnp.float32)).astype(jnp.bfloat16)
    gx = lax.axis_index("gx")
    own_cols = lax.dynamic_slice_in_dim(normed, gx * width_part, width_part, 1)
    partner_gx = (gx + 2) % 4
    sent = lax.dynamic_slice_in_dim(normed, partner_gx * width_part, width_part, 1)
    got = lax.ppermute(sent, ALL, neighbour_pairs())
    zh = lax.axis_index("zh")
    pair = jnp.zeros((2,) + own_cols.shape, own_cols.dtype)
    pair = lax.dynamic_update_index_in_dim(pair, own_cols, zh, 0)
    pair = lax.dynamic_update_index_in_dim(pair, got, 1 - zh, 0)
    first = pair[..., : width_part // 2]
    second = pair[..., width_part // 2 :]
    first = direct_all_gather(first, "y", 4, 0)
    second = direct_all_gather(second, "x", 4, 0)
    half = width_part // 2

    def project(lo, hi):
        return lambda piece: jnp.concatenate(
            [
                jnp.dot(piece, w_query[lo:hi], preferred_element_type=jnp.float32),
                jnp.dot(piece, w_keyval[lo:hi], preferred_element_type=jnp.float32),
            ],
            axis=-1,
        )

    projected = ring_all_gather_apply(first, "x", 4, 0, project(0, half))
    projected = projected + ring_all_gather_apply(second, "y", 4, 1, project(half, width_part))
    projected = projected.reshape(-1, query_cols + pair_cols)
    projected = projected.reshape(4, 4, 2, -1, projected.shape[1]).transpose(2, 0, 1, 3, 4)
    projected = projected.reshape(-1, projected.shape[-1])
    arrived = lax.all_to_all(projected.astype(jnp.bfloat16), ALL, split_axis=0, concat_axis=0, tiled=True)
    rows_dev = arrived.shape[0] // 128
    summed = arrived.reshape(4, peers, rows_dev, query_cols + pair_cols).astype(jnp.float32).sum(axis=0)
    split_cols = summed.astype(jnp.bfloat16).transpose(1, 0, 2)
    query = split_cols[:, :, :query_cols].reshape(rows_dev, peers * query_cols)
    keyval = split_cols[:, :, query_cols:].reshape(rows_dev, peers * pair_cols)
    attended = attend_rows(query, keyval, key_cache, value_cache, lengths)
    heads_first = attended.reshape(rows_dev, peers, query_cols).transpose(1, 0, 2)
    sent = jnp.broadcast_to(heads_first[None], (4,) + heads_first.shape).reshape(-1, query_cols)
    full_rows = lax.all_to_all(sent, ALL, split_axis=0, concat_axis=0, tiled=True)
    cols = w_out.shape[1]
    by_row = full_rows.reshape(2, 4, 4, rows_dev * 4, query_cols)

    def partial_out(dim, lo, hi):
        return lambda k: jnp.dot(
            lax.dynamic_index_in_dim(by_row, k, dim, keepdims=False),
            w_out[:, lo:hi],
            preferred_element_type=jnp.float32,
        ).astype(jnp.bfloat16)

    first = ring_reduce_scatter(partial_out(2, 0, cols // 2), "y", 4)
    second = ring_reduce_scatter(partial_out(1, cols // 2, cols), "x", 4)
    first = direct_reduce_scatter(blocks_of(first, 1), "x", 4)
    second = direct_reduce_scatter(blocks_of(second, 1), "y", 4)
    first = ring_reduce_scatter(blocks_of(first, 0), "zh", 2)
    second = ring_reduce_scatter(blocks_of(second, 0), "zh", 2)
    return jnp.concatenate([first, second], axis=-1)


def solution(mesh):
    from jax.sharding import Mesh
    mesh = Mesh(mesh.devices.reshape(4, 2, 4, 4), ("gx", "zh", "x", "y"))
    in_specs = (
        P(GY, None),
        P(),
        P("gx", GY),
        P("gx", GY),
        P(("gx",) + GY, None, None, None),
        P(("gx",) + GY, None, None, None),
        P(("gx",) + GY),
        P(GY, "gx"),
    )
    out_specs = P(GY, "gx")
    return jax.shard_map(shards, mesh=mesh, in_specs=in_specs, out_specs=out_specs, check_vma=False)
```

```python
import math

import jax
import jax.numpy as jnp
from jax import lax
from jax.sharding import PartitionSpec as P

GY = ("zh", "x", "y")
ALL = ("gx",) + GY


def rotate_heads(values, position, head_dim):
    half = head_dim // 2
    freq = jnp.exp(-(jnp.arange(half, dtype=jnp.float32) * 2.0 / head_dim) * math.log(500000.0))
    angle = position[:, None] * freq[None, :]
    cosine = jnp.cos(angle)[:, None, :]
    sine = jnp.sin(angle)[:, None, :]
    first = values[..., :half]
    second = values[..., half:]
    return jnp.concatenate(
        [first * cosine - second * sine, second * cosine + first * sine], axis=-1
    )


def attend_rows(query, keyval, key_cache, value_cache, lengths):
    rows, cache_len, kv_heads, head_dim = key_cache.shape
    heads = query.shape[1] // head_dim
    group = heads // kv_heads
    scale = 1.0 / math.sqrt(head_dim)
    position = lengths.astype(jnp.float32)
    rotated = rotate_heads(
        query.astype(jnp.float32).reshape(rows, heads, head_dim), position, head_dim
    ).astype(jnp.bfloat16)
    pairs = keyval.reshape(rows, 2, kv_heads, head_dim)
    new_key = rotate_heads(pairs[:, 0].astype(jnp.float32), position, head_dim).astype(jnp.bfloat16)
    new_value = pairs[:, 1].astype(jnp.float32)
    grouped = rotated.reshape(rows, kv_heads, group, head_dim)
    scores = (
        jnp.einsum("rgqd,rtgd->rgqt", grouped, key_cache, preferred_element_type=jnp.float32)
        * scale
    )
    own = jnp.einsum("rgqd,rgd->rgq", grouped, new_key, preferred_element_type=jnp.float32) * scale
    valid = jnp.arange(cache_len)[None, None, None, :] < lengths[:, None, None, None]
    scores = jnp.where(valid, scores, -jnp.inf)
    top = jnp.maximum(jnp.max(scores, axis=-1), own)
    weights = jnp.exp(scores - top[..., None])
    own_weight = jnp.exp(own - top)
    total = jnp.sum(weights, axis=-1) + own_weight
    probs = (weights / total[..., None]).astype(jnp.bfloat16)
    own_prob = (own_weight / total).astype(jnp.bfloat16)
    result = jnp.einsum("rgqt,rtgd->rgqd", probs, value_cache, preferred_element_type=jnp.float32)
    result = result + own_prob.astype(jnp.float32)[..., None] * new_value[:, :, None, :]
    return result.astype(jnp.bfloat16).reshape(rows, heads * head_dim)


def ring_all_gather(blk, axis, n, dim):
    idx = lax.axis_index(axis)
    fwd = [(i, (i + 1) % n) for i in range(n)]
    bwd = [(i, (i - 1) % n) for i in range(n)]
    out = jnp.zeros(blk.shape[:dim] + (n,) + blk.shape[dim:], blk.dtype)
    out = lax.dynamic_update_index_in_dim(out, blk, idx, dim)
    from_left = lax.ppermute(blk, axis, fwd)
    out = lax.dynamic_update_index_in_dim(out, from_left, (idx - 1) % n, dim)
    if n == 2:
        return out
    from_right = lax.ppermute(blk, axis, bwd)
    out = lax.dynamic_update_index_in_dim(out, from_right, (idx + 1) % n, dim)
    half = blk.shape[-1] // 2
    first = lax.ppermute(from_left[..., :half], axis, fwd)
    second = lax.ppermute(from_right[..., half:], axis, bwd)
    opposite = jnp.concatenate([first, second], axis=-1)
    return lax.dynamic_update_index_in_dim(out, opposite, (idx + 2) % n, dim)


def ring_all_gather_apply(blk, axis, n, dim, fn):
    idx = lax.axis_index(axis)
    fwd = [(i, (i + 1) % n) for i in range(n)]
    bwd = [(i, (i - 1) % n) for i in range(n)]
    from_left = lax.ppermute(blk, axis, fwd)
    from_right = lax.ppermute(blk, axis, bwd)
    own = fn(blk)
    out = jnp.zeros(own.shape[:dim] + (n,) + own.shape[dim:], own.dtype)
    out = lax.dynamic_update_index_in_dim(out, own, idx, dim)
    half = blk.shape[-1] // 2
    first = lax.ppermute(from_left[..., :half], axis, fwd)
    second = lax.ppermute(from_right[..., half:], axis, bwd)
    out = lax.dynamic_update_index_in_dim(out, fn(from_left), (idx - 1) % n, dim)
    out = lax.dynamic_update_index_in_dim(out, fn(from_right), (idx + 1) % n, dim)
    opposite = jnp.concatenate([first, second], axis=-1)
    return lax.dynamic_update_index_in_dim(out, fn(opposite), (idx + 2) % n, dim)


def blocks_of(arr, dim):
    return lambda k: lax.dynamic_index_in_dim(arr, k, dim, keepdims=False)


def ring_reduce_scatter(make, axis, n):
    idx = lax.axis_index(axis)

    def take(k):
        return make(k % n)

    fwd = [(i, (i + 1) % n) for i in range(n)]
    bwd = [(i, (i - 1) % n) for i in range(n)]
    if n == 2:
        return take(idx) + lax.ppermute(take(idx + 1), axis, fwd)
    opposite = take(idx + 2)
    half = opposite.shape[-1] // 2
    from_right = lax.ppermute(opposite[..., :half], axis, bwd)
    from_left = lax.ppermute(opposite[..., half:], axis, fwd)
    to_left = take(idx - 1)
    to_left = jnp.concatenate([to_left[..., :half] + from_right, to_left[..., half:]], axis=-1)
    to_right = take(idx + 1)
    to_right = jnp.concatenate([to_right[..., :half], to_right[..., half:] + from_left], axis=-1)
    got_right = lax.ppermute(to_left, axis, bwd)
    got_left = lax.ppermute(to_right, axis, fwd)
    return take(idx) + got_right + got_left


def neighbour_pairs():
    pairs = []
    for gx in range(4):
        for gy in range(32):
            pairs.append((gx * 32 + gy, ((gx + 2) % 4) * 32 + (gy + 16) % 32))
    return pairs


def shards(hidden, norm_gain, w_query, w_keyval, key_cache, value_cache, lengths, w_out):
    width_part = w_query.shape[0]
    query_cols = w_query.shape[1]
    pair_cols = w_keyval.shape[1]
    peers = 32
    values = hidden.astype(jnp.float32)
    inverse = lax.rsqrt(jnp.mean(values * values, axis=1, keepdims=True) + 1e-05)
    normed = (values * inverse * norm_gain.astype(jnp.float32)).astype(jnp.bfloat16)
    gx = lax.axis_index("gx")
    own_cols = lax.dynamic_slice_in_dim(normed, gx * width_part, width_part, 1)
    partner_gx = (gx + 2) % 4
    sent = lax.dynamic_slice_in_dim(normed, partner_gx * width_part, width_part, 1)
    got = lax.ppermute(sent, ALL, neighbour_pairs())
    zh = lax.axis_index("zh")
    pair = jnp.zeros((2,) + own_cols.shape, own_cols.dtype)
    pair = lax.dynamic_update_index_in_dim(pair, own_cols, zh, 0)
    pair = lax.dynamic_update_index_in_dim(pair, got, 1 - zh, 0)
    first = pair[..., : width_part // 2]
    second = pair[..., width_part // 2 :]
    first = ring_all_gather(first, "y", 4, 0)
    second = ring_all_gather(second, "x", 4, 0)
    half = width_part // 2

    def project(lo, hi):
        return lambda piece: jnp.concatenate(
            [
                jnp.dot(piece, w_query[lo:hi], preferred_element_type=jnp.float32),
                jnp.dot(piece, w_keyval[lo:hi], preferred_element_type=jnp.float32),
            ],
            axis=-1,
        )

    projected = ring_all_gather_apply(first, "x", 4, 0, project(0, half))
    projected = projected + ring_all_gather_apply(second, "y", 4, 1, project(half, width_part))
    projected = projected.reshape(-1, query_cols + pair_cols)
    projected = projected.reshape(4, 4, 2, -1, projected.shape[1]).transpose(2, 0, 1, 3, 4)
    projected = projected.reshape(-1, projected.shape[-1])
    arrived = lax.all_to_all(projected.astype(jnp.bfloat16), ALL, split_axis=0, concat_axis=0, tiled=True)
    rows_dev = arrived.shape[0] // 128
    summed = arrived.reshape(4, peers, rows_dev, query_cols + pair_cols).astype(jnp.float32).sum(axis=0)
    split_cols = summed.astype(jnp.bfloat16).transpose(1, 0, 2)
    query = split_cols[:, :, :query_cols].reshape(rows_dev, peers * query_cols)
    keyval = split_cols[:, :, query_cols:].reshape(rows_dev, peers * pair_cols)
    attended = attend_rows(query, keyval, key_cache, value_cache, lengths)
    by_heads = lax.all_to_all(attended, GY, split_axis=1, concat_axis=0, tiled=True)
    full_rows = ring_all_gather(by_heads, "gx", 4, 0).reshape(-1, query_cols)
    cols = w_out.shape[1]
    by_row = full_rows.reshape(2, 4, 4, rows_dev * 4, query_cols)

    def partial_out(dim, lo, hi):
        return lambda k: jnp.dot(
            lax.dynamic_index_in_dim(by_row, k, dim, keepdims=False),
            w_out[:, lo:hi],
            preferred_element_type=jnp.float32,
        ).astype(jnp.bfloat16)

    first = ring_reduce_scatter(partial_out(2, 0, cols // 2), "y", 4)
    second = ring_reduce_scatter(partial_out(1, cols // 2, cols), "x", 4)
    first = ring_reduce_scatter(blocks_of(first, 1), "x", 4)
    second = ring_reduce_scatter(blocks_of(second, 1), "y", 4)
    first = ring_reduce_scatter(blocks_of(first, 0), "zh", 2)
    second = ring_reduce_scatter(blocks_of(second, 0), "zh", 2)
    return jnp.concatenate([first, second], axis=-1)


def solution(mesh):
    from jax.sharding import Mesh
    mesh = Mesh(mesh.devices.reshape(4, 2, 4, 4), ("gx", "zh", "x", "y"))
    in_specs = (
        P(GY, None),
        P(),
        P("gx", GY),
        P("gx", GY),
        P(("gx",) + GY, None, None, None),
        P(("gx",) + GY, None, None, None),
        P(("gx",) + GY),
        P(GY, "gx"),
    )
    out_specs = P(GY, "gx")
    return jax.shard_map(shards, mesh=mesh, in_specs=in_specs, out_specs=out_specs, check_vma=False)
```

```python
import math

import jax
import jax.numpy as jnp
from jax import lax
from jax.sharding import PartitionSpec as P

GY = ("zh", "x", "y")
ALL = ("gx",) + GY


def rotate_heads(values, position, head_dim):
    half = head_dim // 2
    freq = jnp.exp(-(jnp.arange(half, dtype=jnp.float32) * 2.0 / head_dim) * math.log(500000.0))
    angle = position[:, None] * freq[None, :]
    cosine = jnp.cos(angle)[:, None, :]
    sine = jnp.sin(angle)[:, None, :]
    first = values[..., :half]
    second = values[..., half:]
    return jnp.concatenate(
        [first * cosine - second * sine, second * cosine + first * sine], axis=-1
    )


def attend_rows(query, keyval, key_cache, value_cache, lengths):
    rows, cache_len, kv_heads, head_dim = key_cache.shape
    heads = query.shape[1] // head_dim
    group = heads // kv_heads
    scale = 1.0 / math.sqrt(head_dim)
    position = lengths.astype(jnp.float32)
    rotated = rotate_heads(
        query.astype(jnp.float32).reshape(rows, heads, head_dim), position, head_dim
    ).astype(jnp.bfloat16)
    pairs = keyval.reshape(rows, 2, kv_heads, head_dim)
    new_key = rotate_heads(pairs[:, 0].astype(jnp.float32), position, head_dim).astype(jnp.bfloat16)
    new_value = pairs[:, 1].astype(jnp.float32)
    grouped = rotated.reshape(rows, kv_heads, group, head_dim)
    scores = (
        jnp.einsum("rgqd,rtgd->rgqt", grouped, key_cache, preferred_element_type=jnp.float32)
        * scale
    )
    own = jnp.einsum("rgqd,rgd->rgq", grouped, new_key, preferred_element_type=jnp.float32) * scale
    valid = jnp.arange(cache_len)[None, None, None, :] < lengths[:, None, None, None]
    scores = jnp.where(valid, scores, -jnp.inf)
    top = jnp.maximum(jnp.max(scores, axis=-1), own)
    weights = jnp.exp(scores - top[..., None])
    own_weight = jnp.exp(own - top)
    total = jnp.sum(weights, axis=-1) + own_weight
    probs = (weights / total[..., None]).astype(jnp.bfloat16)
    own_prob = (own_weight / total).astype(jnp.bfloat16)
    result = jnp.einsum("rgqt,rtgd->rgqd", probs, value_cache, preferred_element_type=jnp.float32)
    result = result + own_prob.astype(jnp.float32)[..., None] * new_value[:, :, None, :]
    return result.astype(jnp.bfloat16).reshape(rows, heads * head_dim)


def ring_all_gather(blk, axis, n, dim):
    idx = lax.axis_index(axis)
    fwd = [(i, (i + 1) % n) for i in range(n)]
    bwd = [(i, (i - 1) % n) for i in range(n)]
    out = jnp.zeros(blk.shape[:dim] + (n,) + blk.shape[dim:], blk.dtype)
    out = lax.dynamic_update_index_in_dim(out, blk, idx, dim)
    from_left = lax.ppermute(blk, axis, fwd)
    out = lax.dynamic_update_index_in_dim(out, from_left, (idx - 1) % n, dim)
    if n == 2:
        return out
    from_right = lax.ppermute(blk, axis, bwd)
    out = lax.dynamic_update_index_in_dim(out, from_right, (idx + 1) % n, dim)
    half = blk.shape[-1] // 2
    first = lax.ppermute(from_left[..., :half], axis, fwd)
    second = lax.ppermute(from_right[..., half:], axis, bwd)
    opposite = jnp.concatenate([first, second], axis=-1)
    return lax.dynamic_update_index_in_dim(out, opposite, (idx + 2) % n, dim)


def ring_all_gather_apply(blk, axis, n, dim, fn):
    idx = lax.axis_index(axis)
    fwd = [(i, (i + 1) % n) for i in range(n)]
    bwd = [(i, (i - 1) % n) for i in range(n)]
    from_left = lax.ppermute(blk, axis, fwd)
    from_right = lax.ppermute(blk, axis, bwd)
    own = fn(blk)
    out = jnp.zeros(own.shape[:dim] + (n,) + own.shape[dim:], own.dtype)
    out = lax.dynamic_update_index_in_dim(out, own, idx, dim)
    half = blk.shape[-1] // 2
    first = lax.ppermute(from_left[..., :half], axis, fwd)
    second = lax.ppermute(from_right[..., half:], axis, bwd)
    out = lax.dynamic_update_index_in_dim(out, fn(from_left), (idx - 1) % n, dim)
    out = lax.dynamic_update_index_in_dim(out, fn(from_right), (idx + 1) % n, dim)
    opposite = jnp.concatenate([first, second], axis=-1)
    return lax.dynamic_update_index_in_dim(out, fn(opposite), (idx + 2) % n, dim)


def blocks_of(arr, dim):
    return lambda k: lax.dynamic_index_in_dim(arr, k, dim, keepdims=False)


def ring_reduce_scatter(make, axis, n):
    idx = lax.axis_index(axis)

    def take(k):
        return make(k % n)

    fwd = [(i, (i + 1) % n) for i in range(n)]
    bwd = [(i, (i - 1) % n) for i in range(n)]
    if n == 2:
        return take(idx) + lax.ppermute(take(idx + 1), axis, fwd)
    opposite = take(idx + 2)
    half = opposite.shape[-1] // 2
    from_right = lax.ppermute(opposite[..., :half], axis, bwd)
    from_left = lax.ppermute(opposite[..., half:], axis, fwd)
    to_left = take(idx - 1)
    to_left = jnp.concatenate([to_left[..., :half] + from_right, to_left[..., half:]], axis=-1)
    to_right = take(idx + 1)
    to_right = jnp.concatenate([to_right[..., :half], to_right[..., half:] + from_left], axis=-1)
    got_right = lax.ppermute(to_left, axis, bwd)
    got_left = lax.ppermute(to_right, axis, fwd)
    return take(idx) + got_right + got_left


def neighbour_pairs():
    pairs = []
    for gx in range(4):
        for gy in range(32):
            pairs.append((gx * 32 + gy, ((gx + 2) % 4) * 32 + (gy + 16) % 32))
    return pairs


def shards(hidden, norm_gain, w_query, w_keyval, key_cache, value_cache, lengths, w_out):
    width_part = w_query.shape[0]
    query_cols = w_query.shape[1]
    pair_cols = w_keyval.shape[1]
    peers = 32
    values = hidden.astype(jnp.float32)
    inverse = lax.rsqrt(jnp.mean(values * values, axis=1, keepdims=True) + 1e-05)
    normed = (values * inverse * norm_gain.astype(jnp.float32)).astype(jnp.bfloat16)
    gx = lax.axis_index("gx")
    own_cols = lax.dynamic_slice_in_dim(normed, gx * width_part, width_part, 1)
    partner_gx = (gx + 2) % 4
    sent = lax.dynamic_slice_in_dim(normed, partner_gx * width_part, width_part, 1)
    got = lax.ppermute(sent, ALL, neighbour_pairs())
    zh = lax.axis_index("zh")
    pair = jnp.zeros((2,) + own_cols.shape, own_cols.dtype)
    pair = lax.dynamic_update_index_in_dim(pair, own_cols, zh, 0)
    pair = lax.dynamic_update_index_in_dim(pair, got, 1 - zh, 0)
    first = pair[..., : width_part // 2]
    second = pair[..., width_part // 2 :]
    first = ring_all_gather(first, "y", 4, 0)
    second = ring_all_gather(second, "x", 4, 0)
    half = width_part // 2

    def project(lo, hi):
        return lambda piece: jnp.concatenate(
            [
                jnp.dot(piece, w_query[lo:hi], preferred_element_type=jnp.float32),
                jnp.dot(piece, w_keyval[lo:hi], preferred_element_type=jnp.float32),
            ],
            axis=-1,
        )

    projected = ring_all_gather_apply(first, "x", 4, 0, project(0, half))
    projected = projected + ring_all_gather_apply(second, "y", 4, 1, project(half, width_part))
    projected = projected.reshape(-1, query_cols + pair_cols)
    projected = projected.reshape(4, 4, 2, -1, projected.shape[1]).transpose(2, 0, 1, 3, 4)
    projected = projected.reshape(-1, projected.shape[-1])
    summed = ring_reduce_scatter(blocks_of(projected.reshape(4, -1, projected.shape[-1]), 0), "gx", 4)
    local_qkv = lax.all_to_all(summed.astype(jnp.bfloat16), GY, split_axis=0, concat_axis=1, tiled=True)
    rows_dev = local_qkv.shape[0]
    split_cols = local_qkv.reshape(rows_dev, peers, query_cols + pair_cols)
    query = split_cols[:, :, :query_cols].reshape(rows_dev, peers * query_cols)
    keyval = split_cols[:, :, query_cols:].reshape(rows_dev, peers * pair_cols)
    attended = attend_rows(query, keyval, key_cache, value_cache, lengths)
    by_heads = lax.all_to_all(attended, GY, split_axis=1, concat_axis=0, tiled=True)
    full_rows = ring_all_gather(by_heads, "gx", 4, 0).reshape(-1, query_cols)
    cols = w_out.shape[1]
    by_row = full_rows.reshape(2, 4, 4, rows_dev * 4, query_cols)

    def partial_out(dim, lo, hi):
        return lambda k: jnp.dot(
            lax.dynamic_index_in_dim(by_row, k, dim, keepdims=False),
            w_out[:, lo:hi],
            preferred_element_type=jnp.float32,
        ).astype(jnp.bfloat16)

    first = ring_reduce_scatter(partial_out(2, 0, cols // 2), "y", 4)
    second = ring_reduce_scatter(partial_out(1, cols // 2, cols), "x", 4)
    first = ring_reduce_scatter(blocks_of(first, 1), "x", 4)
    second = ring_reduce_scatter(blocks_of(second, 1), "y", 4)
    first = ring_reduce_scatter(blocks_of(first, 0), "zh", 2)
    second = ring_reduce_scatter(blocks_of(second, 0), "zh", 2)
    return jnp.concatenate([first, second], axis=-1)


def solution(mesh):
    from jax.sharding import Mesh
    mesh = Mesh(mesh.devices.reshape(4, 2, 4, 4), ("gx", "zh", "x", "y"))
    in_specs = (
        P(GY, None),
        P(),
        P("gx", GY),
        P("gx", GY),
        P(("gx",) + GY, None, None, None),
        P(("gx",) + GY, None, None, None),
        P(("gx",) + GY),
        P(GY, "gx"),
    )
    out_specs = P(GY, "gx")
    return jax.shard_map(shards, mesh=mesh, in_specs=in_specs, out_specs=out_specs, check_vma=False)
```

```python
import math

import jax
import jax.numpy as jnp
from jax import lax
from jax.sharding import PartitionSpec as P

GY = ("zh", "x", "y")
ALL = ("gx",) + GY


def rotate_heads(values, position, head_dim):
    half = head_dim // 2
    freq = jnp.exp(-(jnp.arange(half, dtype=jnp.float32) * 2.0 / head_dim) * math.log(500000.0))
    angle = position[:, None] * freq[None, :]
    cosine = jnp.cos(angle)[:, None, :]
    sine = jnp.sin(angle)[:, None, :]
    first = values[..., :half]
    second = values[..., half:]
    return jnp.concatenate(
        [first * cosine - second * sine, second * cosine + first * sine], axis=-1
    )


def attend_rows(query, keyval, key_cache, value_cache, lengths):
    rows, cache_len, kv_heads, head_dim = key_cache.shape
    heads = query.shape[1] // head_dim
    group = heads // kv_heads
    scale = 1.0 / math.sqrt(head_dim)
    position = lengths.astype(jnp.float32)
    rotated = rotate_heads(
        query.astype(jnp.float32).reshape(rows, heads, head_dim), position, head_dim
    ).astype(jnp.bfloat16)
    pairs = keyval.reshape(rows, 2, kv_heads, head_dim)
    new_key = rotate_heads(pairs[:, 0].astype(jnp.float32), position, head_dim).astype(jnp.bfloat16)
    new_value = pairs[:, 1].astype(jnp.float32)
    grouped = rotated.reshape(rows, kv_heads, group, head_dim)
    scores = (
        jnp.einsum("rgqd,rtgd->rgqt", grouped, key_cache, preferred_element_type=jnp.float32)
        * scale
    )
    own = jnp.einsum("rgqd,rgd->rgq", grouped, new_key, preferred_element_type=jnp.float32) * scale
    valid = jnp.arange(cache_len)[None, None, None, :] < lengths[:, None, None, None]
    scores = jnp.where(valid, scores, -jnp.inf)
    top = jnp.maximum(jnp.max(scores, axis=-1), own)
    weights = jnp.exp(scores - top[..., None])
    own_weight = jnp.exp(own - top)
    total = jnp.sum(weights, axis=-1) + own_weight
    probs = (weights / total[..., None]).astype(jnp.bfloat16)
    own_prob = (own_weight / total).astype(jnp.bfloat16)
    result = jnp.einsum("rgqt,rtgd->rgqd", probs, value_cache, preferred_element_type=jnp.float32)
    result = result + own_prob.astype(jnp.float32)[..., None] * new_value[:, :, None, :]
    return result.astype(jnp.bfloat16).reshape(rows, heads * head_dim)


def ring_all_gather(blk, axis, n, dim):
    idx = lax.axis_index(axis)
    fwd = [(i, (i + 1) % n) for i in range(n)]
    bwd = [(i, (i - 1) % n) for i in range(n)]
    out = jnp.zeros(blk.shape[:dim] + (n,) + blk.shape[dim:], blk.dtype)
    out = lax.dynamic_update_index_in_dim(out, blk, idx, dim)
    from_left = lax.ppermute(blk, axis, fwd)
    out = lax.dynamic_update_index_in_dim(out, from_left, (idx - 1) % n, dim)
    if n == 2:
        return out
    from_right = lax.ppermute(blk, axis, bwd)
    out = lax.dynamic_update_index_in_dim(out, from_right, (idx + 1) % n, dim)
    half = blk.shape[-1] // 2
    first = lax.ppermute(from_left[..., :half], axis, fwd)
    second = lax.ppermute(from_right[..., half:], axis, bwd)
    opposite = jnp.concatenate([first, second], axis=-1)
    return lax.dynamic_update_index_in_dim(out, opposite, (idx + 2) % n, dim)


def direct_all_gather(blk, axis, n, dim):
    idx = lax.axis_index(axis)
    out = jnp.zeros(blk.shape[:dim] + (n,) + blk.shape[dim:], blk.dtype)
    out = lax.dynamic_update_index_in_dim(out, blk, idx, dim)
    for d in range(1, n):
        got = lax.ppermute(blk, axis, [(i, (i + d) % n) for i in range(n)])
        out = lax.dynamic_update_index_in_dim(out, got, (idx - d) % n, dim)
    return out


def ring_all_gather_apply(blk, axis, n, dim, fn):
    idx = lax.axis_index(axis)
    fwd = [(i, (i + 1) % n) for i in range(n)]
    bwd = [(i, (i - 1) % n) for i in range(n)]
    from_left = lax.ppermute(blk, axis, fwd)
    from_right = lax.ppermute(blk, axis, bwd)
    own = fn(blk)
    out = jnp.zeros(own.shape[:dim] + (n,) + own.shape[dim:], own.dtype)
    out = lax.dynamic_update_index_in_dim(out, own, idx, dim)
    half = blk.shape[-1] // 2
    first = lax.ppermute(from_left[..., :half], axis, fwd)
    second = lax.ppermute(from_right[..., half:], axis, bwd)
    out = lax.dynamic_update_index_in_dim(out, fn(from_left), (idx - 1) % n, dim)
    out = lax.dynamic_update_index_in_dim(out, fn(from_right), (idx + 1) % n, dim)
    opposite = jnp.concatenate([first, second], axis=-1)
    return lax.dynamic_update_index_in_dim(out, fn(opposite), (idx + 2) % n, dim)


def blocks_of(arr, dim):
    return lambda k: lax.dynamic_index_in_dim(arr, k, dim, keepdims=False)


def ring_reduce_scatter(make, axis, n):
    idx = lax.axis_index(axis)

    def take(k):
        return make(k % n)

    fwd = [(i, (i + 1) % n) for i in range(n)]
    bwd = [(i, (i - 1) % n) for i in range(n)]
    if n == 2:
        return take(idx) + lax.ppermute(take(idx + 1), axis, fwd)
    opposite = take(idx + 2)
    half = opposite.shape[-1] // 2
    from_right = lax.ppermute(opposite[..., :half], axis, bwd)
    from_left = lax.ppermute(opposite[..., half:], axis, fwd)
    to_left = take(idx - 1)
    to_left = jnp.concatenate([to_left[..., :half] + from_right, to_left[..., half:]], axis=-1)
    to_right = take(idx + 1)
    to_right = jnp.concatenate([to_right[..., :half], to_right[..., half:] + from_left], axis=-1)
    got_right = lax.ppermute(to_left, axis, bwd)
    got_left = lax.ppermute(to_right, axis, fwd)
    return take(idx) + got_right + got_left


def neighbour_pairs():
    pairs = []
    for gx in range(4):
        for gy in range(32):
            pairs.append((gx * 32 + gy, ((gx + 2) % 4) * 32 + (gy + 16) % 32))
    return pairs


def shards(hidden, norm_gain, w_query, w_keyval, key_cache, value_cache, lengths, w_out):
    width_part = w_query.shape[0]
    query_cols = w_query.shape[1]
    pair_cols = w_keyval.shape[1]
    peers = 32
    values = hidden.astype(jnp.float32)
    inverse = lax.rsqrt(jnp.mean(values * values, axis=1, keepdims=True) + 1e-05)
    normed = (values * inverse * norm_gain.astype(jnp.float32)).astype(jnp.bfloat16)
    gx = lax.axis_index("gx")
    own_cols = lax.dynamic_slice_in_dim(normed, gx * width_part, width_part, 1)
    partner_gx = (gx + 2) % 4
    sent = lax.dynamic_slice_in_dim(normed, partner_gx * width_part, width_part, 1)
    got = lax.ppermute(sent, ALL, neighbour_pairs())
    zh = lax.axis_index("zh")
    pair = jnp.zeros((2,) + own_cols.shape, own_cols.dtype)
    pair = lax.dynamic_update_index_in_dim(pair, own_cols, zh, 0)
    pair = lax.dynamic_update_index_in_dim(pair, got, 1 - zh, 0)
    first = pair[..., : width_part // 2]
    second = pair[..., width_part // 2 :]
    first = ring_all_gather(first, "y", 4, 0)
    second = ring_all_gather(second, "x", 4, 0)
    half = width_part // 2

    def project(lo, hi):
        return lambda piece: jnp.concatenate(
            [
                jnp.dot(piece, w_query[lo:hi], preferred_element_type=jnp.float32),
                jnp.dot(piece, w_keyval[lo:hi], preferred_element_type=jnp.float32),
            ],
            axis=-1,
        )

    projected = ring_all_gather_apply(first, "x", 4, 0, project(0, half))
    projected = projected + ring_all_gather_apply(second, "y", 4, 1, project(half, width_part))
    projected = projected.reshape(-1, query_cols + pair_cols)
    projected = projected.reshape(4, 4, 2, -1, projected.shape[1]).transpose(2, 0, 1, 3, 4)
    projected = projected.reshape(-1, projected.shape[-1])
    arrived = lax.all_to_all(projected.astype(jnp.bfloat16), ALL, split_axis=0, concat_axis=0, tiled=True)
    rows_dev = arrived.shape[0] // 128
    summed = arrived.reshape(4, peers, rows_dev, query_cols + pair_cols).astype(jnp.float32).sum(axis=0)
    split_cols = summed.astype(jnp.bfloat16).transpose(1, 0, 2)
    query = split_cols[:, :, :query_cols].reshape(rows_dev, peers * query_cols)
    keyval = split_cols[:, :, query_cols:].reshape(rows_dev, peers * pair_cols)
    attended = attend_rows(query, keyval, key_cache, value_cache, lengths)
    by_heads = lax.all_to_all(attended, GY, split_axis=1, concat_axis=0, tiled=True)
    full_rows = direct_all_gather(by_heads, "gx", 4, 0).reshape(-1, query_cols)
    cols = w_out.shape[1]
    by_row = full_rows.reshape(2, 4, 4, rows_dev * 4, query_cols)

    def partial_out(dim, lo, hi):
        return lambda k: jnp.dot(
            lax.dynamic_index_in_dim(by_row, k, dim, keepdims=False),
            w_out[:, lo:hi],
            preferred_element_type=jnp.float32,
        ).astype(jnp.bfloat16)

    first = ring_reduce_scatter(partial_out(2, 0, cols // 2), "y", 4)
    second = ring_reduce_scatter(partial_out(1, cols // 2, cols), "x", 4)
    first = ring_reduce_scatter(blocks_of(first, 1), "x", 4)
    second = ring_reduce_scatter(blocks_of(second, 1), "y", 4)
    first = ring_reduce_scatter(blocks_of(first, 0), "zh", 2)
    second = ring_reduce_scatter(blocks_of(second, 0), "zh", 2)
    return jnp.concatenate([first, second], axis=-1)


def solution(mesh):
    from jax.sharding import Mesh
    mesh = Mesh(mesh.devices.reshape(4, 2, 4, 4), ("gx", "zh", "x", "y"))
    in_specs = (
        P(GY, None),
        P(),
        P("gx", GY),
        P("gx", GY),
        P(("gx",) + GY, None, None, None),
        P(("gx",) + GY, None, None, None),
        P(("gx",) + GY),
        P(GY, "gx"),
    )
    out_specs = P(GY, "gx")
    return jax.shard_map(shards, mesh=mesh, in_specs=in_specs, out_specs=out_specs, check_vma=False)
```
